32 devices in a mesh: amp: 8 (over y, x, core), int: 4 (over z).
Axes of the slice: x: 2, y: 2, z: 4, core: 2. Of those that a mesh axis runs over, the one named last changes fastest.
Arguments:
- amplitudes: float32 [768, 512], P('int'), may hold values from -6 to 6
- slab_integrals: float32 [512, 51200], P('int', 'amp'), may hold values from -0.25 to 0.25
- cycle_integrals: float32 [96, 800, 512], P('int', 'amp'), may hold values from -0.03125 to 0.03125
- occ_irrep: int32 [96], replicated, may hold values from 0 to 7
- vir_irrep: int32 [800], replicated, may hold values from 0 to 7
Outputs:
- ladder: float32 [768, 51200], P('int', 'amp')
- cycle: float32 [512, 512], P('int', 'amp')
The draws below stay inside these ranges and needn't reach their ends.
All inputs are finite; a program needn't handle non-finite values.
Results may differ from the reference program's by a relative error of at most 0.00011.
Values sent between devices are 32-bit elements; how exact they have to be, the bound alone decides.
No kernel may reach another device: no remote copies, remote signals or barrier semaphores. Data moves between devices by JAX's collectives and lax.ppermute only.
A program may use at most 64 MiB of HBM per device.

```python
import jax
import jax.numpy as jnp
from jax import lax

NOCC = 96
NVIR = 800
SLAB = 64
IBAT = 8
PW = 512
ROWS = 768


def with_ends(entries, own_key, low, largest):
    dims = entries.shape
    place = [jax.random.randint(jax.random.fold_in(own_key, axis), (), 0, dims[axis]) for axis in range(len(dims))]
    entries = entries.at[tuple(place)].set(low)
    longest = dims.index(max(dims))
    place[longest] = (place[longest] + 1) % dims[longest]
    return entries.at[tuple(place)].set(largest)


def strengthened(array, own_key, source, target, blocks, factor):
    def block_of(axis_at):
        return (jnp.arange(array.shape[axis_at]) // (array.shape[axis_at] // blocks)).reshape((-1,) + (1,) * (array.ndim - 1 - axis_at))

    one_side = jax.random.permutation(own_key, blocks)[block_of(target)]
    other_side = (block_of(target) + blocks // 2) % blocks
    return jnp.where((block_of(source) == one_side) | (block_of(source) == other_side), factor * array, array)


def shard_levels(key, extent, shards, least, largest):
    gain = 1.0
    for position, shards_of in shards:
        heights = jax.random.uniform(jax.random.fold_in(jax.random.fold_in(key, 6), position), (shards_of,), jnp.float32, least / len(shards), largest / len(shards))
        gain = gain * jnp.repeat(jnp.exp(heights), extent[position] // shards_of).reshape((-1,) + (1,) * (len(extent) - 1 - position))
    return gain


def noise(stream_key, shape, width, most, split=(), kind=jnp.bfloat16):
    loudness = shard_levels(stream_key, shape, split, -0.22, 0.18) if split else 1.0
    drawn = jax.random.normal(stream_key, shape, jnp.float32) * width * loudness
    return jnp.minimum(jnp.maximum(drawn, -most), most).astype(kind)


def gaussian_with(rng, extent, width, bound, pieces, heavy, dtype=jnp.bfloat16):
    values = width * jax.random.normal(rng, extent, jnp.float32)
    if pieces:
        values = values * shard_levels(rng, extent, pieces, -0.22, 0.18)
    return jnp.clip(strengthened(values, jax.random.fold_in(rng, 3), *heavy), -bound, bound).astype(dtype)


def setup_inputs(seed: int = 0) -> dict:
    keys = jax.random.split(jax.random.key(seed), 6)
    return {
        "amplitudes": noise(keys[0], (ROWS, PW), 1.0, 6.0, ((0, 4),), jnp.float32),
        "slab_integrals": noise(keys[1], (PW, SLAB * NVIR), PW ** -0.5, 0.25, ((0, 4), (1, 8)), jnp.float32),
        "cycle_integrals": gaussian_with(keys[2], (NOCC, NVIR, IBAT * SLAB), (NOCC * NVIR) ** -0.5, 0.03125, ((0, 4), (1, 8)), (1, 2, 8, 2.0), jnp.float32),
        "occ_irrep": with_ends(jax.random.randint(keys[3], (NOCC,), 0, 8), jax.random.fold_in(keys[3], 1), 0, 7).astype(jnp.int32),
        "vir_irrep": with_ends(jax.random.randint(keys[4], (NVIR,), 0, 8), jax.random.fold_in(keys[4], 1), 0, 7).astype(jnp.int32),
    }


def reference(amplitudes, slab_integrals, cycle_integrals, occ_irrep, vir_irrep):
    ladder = jnp.dot(amplitudes, slab_integrals, precision=lax.Precision.HIGHEST, preferred_element_type=jnp.float32)
    blocks = ladder.reshape(IBAT, NOCC, SLAB, NVIR)
    sums = jnp.einsum("ikac,kcn->ian", blocks, cycle_integrals, precision=lax.Precision.HIGHEST)
    sums = sums.reshape(IBAT * SLAB, IBAT * SLAB)
    labels = jnp.bitwise_xor(occ_irrep[:IBAT][:, None], vir_irrep[:SLAB][None, :]).reshape(-1)
    keep = labels[:, None] == labels[None, :]
    cycle = jnp.where(keep, sums, jnp.zeros_like(sums))
    return ladder, cycle
```

```python
import jax
import jax.numpy as jnp
from jax import lax
from jax.sharding import PartitionSpec as P

HIGHEST = lax.Precision.HIGHEST
CHUNKS = 4


def per_device(amplitudes, slab_integrals, cycle_integrals, occ_irrep, vir_irrep, n_amp, n_int):
    nocc = occ_irrep.shape[0]
    nvir = vir_irrep.shape[0]
    rows, pw = amplitudes.shape
    pw_local = slab_integrals.shape[0]
    i_local = rows // nocc
    ibat = i_local * n_int
    width = slab_integrals.shape[1]
    a_local = width // nvir
    slab = a_local * n_amp
    k_local, c_local, columns = cycle_integrals.shape
    chunks = CHUNKS
    while a_local % chunks:
        chunks -= 1
    a_chunk = a_local // chunks

    t_cyc = lax.all_to_all(
        amplitudes.reshape(i_local, nocc, pw), "int", split_axis=1, concat_axis=0, tiled=True
    ).reshape(ibat * k_local, pw)

    slab3 = slab_integrals.reshape(pw_local, a_local, nvir)
    ladder_chunks = []
    cycle_chunks = []
    for t in range(chunks):
        v = slab3[:, t * a_chunk:(t + 1) * a_chunk, :].reshape(pw_local, a_chunk * nvir)
        v_all = lax.all_gather(v, "int", axis=0, tiled=True)
        ladder_chunks.append(
            jnp.dot(amplitudes, v_all, precision=HIGHEST, preferred_element_type=jnp.float32)
        )
        l_cyc = jnp.dot(t_cyc, v_all, precision=HIGHEST, preferred_element_type=jnp.float32)
        l_cyc = l_cyc.reshape(ibat, k_local, a_chunk, nvir)
        moved = lax.all_to_all(l_cyc, "amp", split_axis=3, concat_axis=2, tiled=True)
        cycle_chunks.append(
            jnp.einsum("ikac,kcn->ian", moved, cycle_integrals, precision=HIGHEST)
        )
    ladder = jnp.concatenate(ladder_chunks, axis=1)

    parts = jnp.stack(cycle_chunks, 0).reshape(chunks, ibat, n_amp, a_chunk, columns)
    parts = parts.transpose(1, 2, 0, 3, 4).reshape(ibat * slab, columns)
    narrowed = lax.psum_scatter(parts, "amp", scatter_dimension=1, tiled=True)
    sums = lax.psum_scatter(narrowed, "int", scatter_dimension=0, tiled=True)

    col_local = sums.shape[1]
    row_start = lax.axis_index("int") * i_local
    batch_labels = lax.dynamic_slice_in_dim(occ_irrep, row_start, i_local, 0)
    slab_labels = vir_irrep[:slab]
    row_labels = jnp.bitwise_xor(batch_labels[:, None], slab_labels[None, :]).reshape(-1)
    col_ids = lax.axis_index("amp") * col_local + jnp.arange(col_local, dtype=jnp.int32)
    col_occ = col_ids // slab
    col_vir = col_ids % slab
    occ_match = col_occ[:, None] == jnp.arange(nocc, dtype=jnp.int32)[None, :]
    vir_match = col_vir[:, None] == jnp.arange(slab, dtype=jnp.int32)[None, :]
    occ_lookup = jnp.sum(jnp.where(occ_match, occ_irrep[None, :], 0), axis=1)
    vir_lookup = jnp.sum(jnp.where(vir_match, slab_labels[None, :], 0), axis=1)
    col_labels = jnp.bitwise_xor(occ_lookup, vir_lookup)
    keep = row_labels[:, None] == col_labels[None, :]
    cycle = jnp.where(keep, sums, jnp.zeros_like(sums))
    return (ladder, cycle)


def solution(mesh):
    n_amp = mesh.shape["amp"]
    n_int = mesh.shape["int"]
    in_specs = (P("int", None), P("int", "amp"), P("int", "amp", None), P(), P())
    out_specs = (P("int", "amp"), P("int", "amp"))

    def body(*args):
        return per_device(*args, n_amp=n_amp, n_int=n_int)

    return jax.shard_map(
        body, mesh=mesh, in_specs=in_specs, out_specs=out_specs, check_vma=False
    )
```

```python
import jax
import jax.numpy as jnp
from jax import lax
from jax.sharding import PartitionSpec as P

HIGHEST = lax.Precision.HIGHEST
CHUNKS = 2


def per_device(amplitudes, slab_integrals, cycle_integrals, occ_irrep, vir_irrep, n_amp, n_int):
    nocc = occ_irrep.shape[0]
    nvir = vir_irrep.shape[0]
    rows, pw = amplitudes.shape
    pw_local = slab_integrals.shape[0]
    i_local = rows // nocc
    ibat = i_local * n_int
    width = slab_integrals.shape[1]
    a_local = width // nvir
    slab = a_local * n_amp
    k_local, c_local, columns = cycle_integrals.shape
    chunks = CHUNKS
    while a_local % chunks:
        chunks -= 1
    a_chunk = a_local // chunks

    t_cyc = lax.all_to_all(
        amplitudes.reshape(i_local, nocc, pw), "int", split_axis=1, concat_axis=0, tiled=True
    ).reshape(ibat * k_local, pw)
    w2 = cycle_integrals.reshape(k_local * c_local, columns)

    slab3 = slab_integrals.reshape(pw_local, a_local, nvir)
    ladder_chunks = []
    cycle_chunks = []
    for t in range(chunks):
        v = slab3[:, t * a_chunk:(t + 1) * a_chunk, :].reshape(pw_local, a_chunk * nvir)
        v_all = lax.all_gather(v, "int", axis=0, tiled=True)
        ladder_chunks.append(
            jnp.dot(amplitudes, v_all, precision=HIGHEST, preferred_element_type=jnp.float32)
        )
        l_cyc = jnp.dot(t_cyc, v_all, precision=HIGHEST, preferred_element_type=jnp.float32)
        l_cyc = l_cyc.reshape(ibat, k_local, a_chunk, n_amp, c_local).transpose(3, 0, 2, 1, 4)
        moved = lax.all_to_all(l_cyc, "amp", split_axis=0, concat_axis=0, tiled=True)
        moved = moved.reshape(n_amp * ibat * a_chunk, k_local * c_local)
        cycle_chunks.append(
            jnp.dot(moved, w2, precision=HIGHEST, preferred_element_type=jnp.float32)
        )
    ladder = jnp.concatenate(ladder_chunks, axis=1)

    parts = jnp.stack(cycle_chunks, 0).reshape(chunks, n_amp, ibat, a_chunk, columns)
    parts = parts.transpose(2, 1, 0, 3, 4).reshape(ibat * slab, columns)
    narrowed = lax.psum_scatter(parts, "amp", scatter_dimension=1, tiled=True)
    sums = lax.psum_scatter(narrowed, "int", scatter_dimension=0, tiled=True)

    col_local = sums.shape[1]
    row_start = lax.axis_index("int") * i_local
    batch_labels = lax.dynamic_slice_in_dim(occ_irrep, row_start, i_local, 0)
    slab_labels = vir_irrep[:slab]
    row_labels = jnp.bitwise_xor(batch_labels[:, None], slab_labels[None, :]).reshape(-1)
    col_ids = lax.axis_index("amp") * col_local + jnp.arange(col_local, dtype=jnp.int32)
    col_occ = col_ids // slab
    col_vir = col_ids % slab
    occ_match = col_occ[:, None] == jnp.arange(nocc, dtype=jnp.int32)[None, :]
    vir_match = col_vir[:, None] == jnp.arange(slab, dtype=jnp.int32)[None, :]
    occ_lookup = jnp.sum(jnp.where(occ_match, occ_irrep[None, :], 0), axis=1)
    vir_lookup = jnp.sum(jnp.where(vir_match, slab_labels[None, :], 0), axis=1)
    col_labels = jnp.bitwise_xor(occ_lookup, vir_lookup)
    keep = row_labels[:, None] == col_labels[None, :]
    cycle = jnp.where(keep, sums, jnp.zeros_like(sums))
    return (ladder, cycle)


def solution(mesh):
    n_amp = mesh.shape["amp"]
    n_int = mesh.shape["int"]
    in_specs = (P("int", None), P("int", "amp"), P("int", "amp", None), P(), P())
    out_specs = (P("int", "amp"), P("int", "amp"))

    def body(*args):
        return per_device(*args, n_amp=n_amp, n_int=n_int)

    return jax.shard_map(
        body, mesh=mesh, in_specs=in_specs, out_specs=out_specs, check_vma=False
    )
```

```python
import jax
import jax.numpy as jnp
from jax import lax
from jax.sharding import PartitionSpec as P

HIGHEST = lax.Precision.HIGHEST
CHUNKS = 2


def per_device(amplitudes, slab_integrals, cycle_integrals, occ_irrep, vir_irrep, n_amp, n_int):
    nocc = occ_irrep.shape[0]
    nvir = vir_irrep.shape[0]
    rows, pw = amplitudes.shape
    pw_local = slab_integrals.shape[0]
    i_local = rows // nocc
    ibat = i_local * n_int
    width = slab_integrals.shape[1]
    a_local = width // nvir
    slab = a_local * n_amp
    k_local, c_local, columns = cycle_integrals.shape
    chunks = CHUNKS
    while a_local % chunks:
        chunks -= 1
    a_chunk = a_local // chunks

    t_cyc = lax.all_to_all(
        amplitudes.reshape(i_local, nocc, pw), "int", split_axis=1, concat_axis=0, tiled=True
    ).reshape(ibat * k_local, pw)
    w2 = cycle_integrals.transpose(1, 0, 2).reshape(c_local * k_local, columns)

    slab3 = slab_integrals.reshape(pw_local, a_local, nvir)
    ladder_chunks = []
    cycle_chunks = []
    for t in range(chunks):
        v = slab3[:, t * a_chunk:(t + 1) * a_chunk, :].reshape(pw_local, a_chunk * nvir)
        v_all = lax.all_gather(v, "int", axis=0, tiled=True)
        if t:
            v_all, ladder_chunks[-1], cycle_chunks[-1] = lax.optimization_barrier(
                (v_all, ladder_chunks[-1], cycle_chunks[-1])
            )
        ladder_chunks.append(
            jnp.dot(amplitudes, v_all, precision=HIGHEST, preferred_element_type=jnp.float32)
        )
        l_cyc = jnp.dot(t_cyc, v_all, precision=HIGHEST, preferred_element_type=jnp.float32)
        l_cyc = l_cyc.reshape(ibat, k_local, a_chunk, n_amp, c_local).transpose(3, 0, 2, 4, 1)
        l_cyc = l_cyc.reshape(n_amp, ibat * a_chunk, c_local * k_local)
        moved = lax.all_to_all(l_cyc, "amp", split_axis=0, concat_axis=0, tiled=True)
        moved = moved.reshape(n_amp * ibat * a_chunk, c_local * k_local)
        cycle_chunks.append(
            jnp.dot(moved, w2, precision=HIGHEST, preferred_element_type=jnp.float32)
        )
    ladder = jnp.concatenate(ladder_chunks, axis=1)

    col_local = columns // n_amp
    parts = jnp.stack(cycle_chunks, 0).reshape(
        chunks, n_amp, n_int, i_local, a_chunk, n_amp, col_local
    )
    parts = parts.transpose(2, 5, 3, 1, 0, 4, 6).reshape(n_int * n_amp, i_local * slab * col_local)
    sums = lax.psum_scatter(parts, ("int", "amp"), scatter_dimension=0, tiled=True)
    sums = sums.reshape(i_local * slab, col_local)

    row_start = lax.axis_index("int") * i_local
    batch_labels = lax.dynamic_slice_in_dim(occ_irrep, row_start, i_local, 0)
    slab_labels = vir_irrep[:slab]
    row_labels = jnp.bitwise_xor(batch_labels[:, None], slab_labels[None, :]).reshape(-1)
    col_ids = lax.axis_index("amp") * col_local + jnp.arange(col_local, dtype=jnp.int32)
    col_occ = col_ids // slab
    col_vir = col_ids % slab
    occ_match = col_occ[:, None] == jnp.arange(nocc, dtype=jnp.int32)[None, :]
    vir_match = col_vir[:, None] == jnp.arange(slab, dtype=jnp.int32)[None, :]
    occ_lookup = jnp.sum(jnp.where(occ_match, occ_irrep[None, :], 0), axis=1)
    vir_lookup = jnp.sum(jnp.where(vir_match, slab_labels[None, :], 0), axis=1)
    col_labels = jnp.bitwise_xor(occ_lookup, vir_lookup)
    keep = row_labels[:, None] == col_labels[None, :]
    cycle = jnp.where(keep, sums, jnp.zeros_like(sums))
    return (ladder, cycle)


def solution(mesh):
    n_amp = mesh.shape["amp"]
    n_int = mesh.shape["int"]
    in_specs = (P("int", None), P("int", "amp"), P("int", "amp", None), P(), P())
    out_specs = (P("int", "amp"), P("int", "amp"))

    def body(*args):
        return per_device(*args, n_amp=n_amp, n_int=n_int)

    return jax.shard_map(
        body, mesh=mesh, in_specs=in_specs, out_specs=out_specs, check_vma=False
    )
```

```python
import jax
import jax.numpy as jnp
from jax import lax
from jax.sharding import PartitionSpec as P

HIGHEST = lax.Precision.HIGHEST
CHUNKS = 3


def per_device(amplitudes, slab_integrals, cycle_integrals, occ_irrep, vir_irrep, n_amp, n_int):
    nocc = occ_irrep.shape[0]
    nvir = vir_irrep.shape[0]
    rows, pw = amplitudes.shape
    pw_local = slab_integrals.shape[0]
    i_local = rows // nocc
    ibat = i_local * n_int
    width = slab_integrals.shape[1]
    a_local = width // nvir
    slab = a_local * n_amp
    k_local, c_local, columns = cycle_integrals.shape
    chunks = min(CHUNKS, a_local)
    sizes = [a_local // chunks + (1 if t < a_local % chunks else 0) for t in range(chunks)]
    starts = [sum(sizes[:t]) for t in range(chunks)]

    t_cyc = lax.all_to_all(
        amplitudes.reshape(i_local, nocc, pw), "int", split_axis=1, concat_axis=0, tiled=True
    ).reshape(ibat * k_local, pw)
    w2 = cycle_integrals.transpose(1, 0, 2).reshape(c_local * k_local, columns)

    slab3 = slab_integrals.reshape(pw_local, a_local, nvir)
    ladder_chunks = []
    cycle_chunks = []
    for t in range(chunks):
        a_chunk = sizes[t]
        v = slab3[:, starts[t]:starts[t] + a_chunk, :].reshape(pw_local, a_chunk * nvir)
        v_all = lax.all_gather(v, "int", axis=0, tiled=True)
        if t:
            v_all, ladder_chunks[-1], cycle_chunks[-1] = lax.optimization_barrier(
                (v_all, ladder_chunks[-1], cycle_chunks[-1])
            )
        ladder_chunks.append(
            jnp.dot(amplitudes, v_all, precision=HIGHEST, preferred_element_type=jnp.float32)
        )
        l_cyc = jnp.dot(t_cyc, v_all, precision=HIGHEST, preferred_element_type=jnp.float32)
        l_cyc = l_cyc.reshape(ibat, k_local, a_chunk, n_amp, c_local).transpose(3, 0, 2, 4, 1)
        l_cyc = l_cyc.reshape(n_amp, ibat * a_chunk, c_local * k_local)
        moved = lax.all_to_all(l_cyc, "amp", split_axis=0, concat_axis=0, tiled=True)
        moved = moved.reshape(n_amp * ibat * a_chunk, c_local * k_local)
        cycle_chunks.append(
            jnp.dot(moved, w2, precision=HIGHEST, preferred_element_type=jnp.float32)
        )
    ladder = jnp.concatenate(ladder_chunks, axis=1)

    parts = jnp.concatenate(
        [c.reshape(n_amp, ibat, sizes[t], columns) for t, c in enumerate(cycle_chunks)], axis=2
    )
    parts = parts.transpose(1, 0, 2, 3).reshape(ibat * slab, columns)
    narrowed = lax.psum_scatter(parts, "amp", scatter_dimension=1, tiled=True)
    sums = lax.psum_scatter(narrowed, "int", scatter_dimension=0, tiled=True)
    col_local = sums.shape[1]

    row_start = lax.axis_index("int") * i_local
    batch_labels = lax.dynamic_slice_in_dim(occ_irrep, row_start, i_local, 0)
    slab_labels = vir_irrep[:slab]
    row_labels = jnp.bitwise_xor(batch_labels[:, None], slab_labels[None, :]).reshape(-1)
    col_ids = lax.axis_index("amp") * col_local + jnp.arange(col_local, dtype=jnp.int32)
    col_occ = col_ids // slab
    col_vir = col_ids % slab
    occ_match = col_occ[:, None] == jnp.arange(nocc, dtype=jnp.int32)[None, :]
    vir_match = col_vir[:, None] == jnp.arange(slab, dtype=jnp.int32)[None, :]
    occ_lookup = jnp.sum(jnp.where(occ_match, occ_irrep[None, :], 0), axis=1)
    vir_lookup = jnp.sum(jnp.where(vir_match, slab_labels[None, :], 0), axis=1)
    col_labels = jnp.bitwise_xor(occ_lookup, vir_lookup)
    keep = row_labels[:, None] == col_labels[None, :]
    cycle = jnp.where(keep, sums, jnp.zeros_like(sums))
    return (ladder, cycle)


def solution(mesh):
    n_amp = mesh.shape["amp"]
    n_int = mesh.shape["int"]
    in_specs = (P("int", None), P("int", "amp"), P("int", "amp", None), P(), P())
    out_specs = (P("int", "amp"), P("int", "amp"))

    def body(*args):
        return per_device(*args, n_amp=n_amp, n_int=n_int)

    return jax.shard_map(
        body, mesh=mesh, in_specs=in_specs, out_specs=out_specs, check_vma=False
    )
```

```python
import jax
import jax.numpy as jnp
from jax import lax
from jax.sharding import PartitionSpec as P

HIGHEST = lax.Precision.HIGHEST


def per_device(amplitudes, slab_integrals, cycle_integrals, occ_irrep, vir_irrep, n_amp, n_int):
    nocc = occ_irrep.shape[0]
    nvir = vir_irrep.shape[0]
    rows, pw = amplitudes.shape
    pw_local = slab_integrals.shape[0]
    i_local = rows // nocc
    ibat = i_local * n_int
    width = slab_integrals.shape[1]
    a_local = width // nvir
    slab = a_local * n_amp
    k_local, c_local, columns = cycle_integrals.shape
    if a_local >= 4:
        sizes = [a_local // 2, a_local - a_local // 2 - 1, 1]
    elif a_local >= 2:
        sizes = [a_local - 1, 1]
    else:
        sizes = [a_local]
    chunks = len(sizes)
    starts = [sum(sizes[:t]) for t in range(chunks)]

    t_cyc = lax.all_to_all(
        amplitudes.reshape(i_local, nocc, pw), "int", split_axis=1, concat_axis=0, tiled=True
    ).reshape(ibat * k_local, pw)
    w2 = cycle_integrals.transpose(1, 0, 2).reshape(c_local * k_local, columns)

    slab3 = slab_integrals.reshape(pw_local, a_local, nvir)
    ladder_chunks = []
    cycle_chunks = []
    for t in range(chunks):
        a_chunk = sizes[t]
        v = slab3[:, starts[t]:starts[t] + a_chunk, :].reshape(pw_local, a_chunk * nvir)
        v_all = lax.all_gather(v, "int", axis=0, tiled=True)
        if t:
            v_all, ladder_chunks[-1], cycle_chunks[-1] = lax.optimization_barrier(
                (v_all, ladder_chunks[-1], cycle_chunks[-1])
            )
        ladder_chunks.append(None)
        if t < chunks - 1:
            ladder_chunks[-1] = jnp.dot(
                amplitudes, v_all, precision=HIGHEST, preferred_element_type=jnp.float32
            )
        l_cyc = jnp.dot(t_cyc, v_all, precision=HIGHEST, preferred_element_type=jnp.float32)
        l_cyc = l_cyc.reshape(ibat, k_local, a_chunk, n_amp, c_local).transpose(3, 0, 2, 4, 1)
        l_cyc = l_cyc.reshape(n_amp, ibat * a_chunk, c_local * k_local)
        moved = lax.all_to_all(l_cyc, "amp", split_axis=0, concat_axis=0, tiled=True)
        if t == chunks - 1:
            ladder_chunks[-1] = jnp.dot(
                amplitudes, v_all, precision=HIGHEST, preferred_element_type=jnp.float32
            )
            ladder = jnp.concatenate(ladder_chunks, axis=1)
            moved, ladder = lax.optimization_barrier((moved, ladder))
        moved = moved.reshape(n_amp * ibat * a_chunk, c_local * k_local)
        partial_sums = jnp.dot(moved, w2, precision=HIGHEST, preferred_element_type=jnp.float32)
        cycle_chunks.append(lax.psum_scatter(partial_sums, "amp", scatter_dimension=1, tiled=True))

    col_local = columns // n_amp
    parts = jnp.concatenate(
        [c.reshape(n_amp, ibat, sizes[t], col_local) for t, c in enumerate(cycle_chunks)], axis=2
    )
    parts = parts.transpose(1, 0, 2, 3).reshape(ibat * slab, col_local)
    sums = lax.psum_scatter(parts, "int", scatter_dimension=0, tiled=True)

    row_start = lax.axis_index("int") * i_local
    batch_labels = lax.dynamic_slice_in_dim(occ_irrep, row_start, i_local, 0)
    slab_labels = vir_irrep[:slab]
    row_labels = jnp.bitwise_xor(batch_labels[:, None], slab_labels[None, :]).reshape(-1)
    col_ids = lax.axis_index("amp") * col_local + jnp.arange(col_local, dtype=jnp.int32)
    col_occ = col_ids // slab
    col_vir = col_ids % slab
    occ_match = col_occ[:, None] == jnp.arange(nocc, dtype=jnp.int32)[None, :]
    vir_match = col_vir[:, None] == jnp.arange(slab, dtype=jnp.int32)[None, :]
    occ_lookup = jnp.sum(jnp.where(occ_match, occ_irrep[None, :], 0), axis=1)
    vir_lookup = jnp.sum(jnp.where(vir_match, slab_labels[None, :], 0), axis=1)
    col_labels = jnp.bitwise_xor(occ_lookup, vir_lookup)
    keep = row_labels[:, None] == col_labels[None, :]
    cycle = jnp.where(keep, sums, jnp.zeros_like(sums))
    return (ladder, cycle)


def solution(mesh):
    n_amp = mesh.shape["amp"]
    n_int = mesh.shape["int"]
    in_specs = (P("int", None), P("int", "amp"), P("int", "amp", None), P(), P())
    out_specs = (P("int", "amp"), P("int", "amp"))

    def body(*args):
        return per_device(*args, n_amp=n_amp, n_int=n_int)

    return jax.shard_map(
        body, mesh=mesh, in_specs=in_specs, out_specs=out_specs, check_vma=False
    )
```

```python
import jax
import jax.numpy as jnp
from jax import lax
from jax.sharding import PartitionSpec as P

HIGHEST = lax.Precision.HIGHEST


def per_device(amplitudes, slab_integrals, cycle_integrals, occ_irrep, vir_irrep, n_amp, n_int):
    nocc = occ_irrep.shape[0]
    nvir = vir_irrep.shape[0]
    rows, pw = amplitudes.shape
    pw_local = slab_integrals.shape[0]
    i_local = rows // nocc
    ibat = i_local * n_int
    width = slab_integrals.shape[1]
    a_local = width // nvir
    slab = a_local * n_amp
    k_local, c_local, columns = cycle_integrals.shape
    if a_local >= 4:
        sizes = [a_local // 2, a_local - a_local // 2 - 1, 1]
    elif a_local >= 2:
        sizes = [a_local - 1, 1]
    else:
        sizes = [a_local]
    chunks = len(sizes)
    starts = [sum(sizes[:t]) for t in range(chunks)]

    t_cyc = lax.all_to_all(
        amplitudes.reshape(i_local, nocc, pw), "int", split_axis=1, concat_axis=0, tiled=True
    ).reshape(ibat * k_local, pw)
    w2 = cycle_integrals.transpose(1, 0, 2).reshape(c_local * k_local, columns)

    slab3 = slab_integrals.reshape(pw_local, a_local, nvir)
    ladder_chunks = []
    cycle_chunks = []
    for t in range(chunks):
        a_chunk = sizes[t]
        v = slab3[:, starts[t]:starts[t] + a_chunk, :].reshape(pw_local, a_chunk * nvir)
        v_all = lax.all_gather(v, "int", axis=0, tiled=True)
        if t:
            v_all, ladder_chunks[-1], cycle_chunks[-1] = lax.optimization_barrier(
                (v_all, ladder_chunks[-1], cycle_chunks[-1])
            )
        ladder_chunks.append(None)
        if t < chunks - 1:
            ladder_chunks[-1] = jnp.dot(
                amplitudes, v_all, precision=HIGHEST, preferred_element_type=jnp.float32
            )
        l_cyc = jnp.dot(t_cyc, v_all, precision=HIGHEST, preferred_element_type=jnp.float32)
        l_cyc = l_cyc.reshape(ibat, k_local, a_chunk, n_amp, c_local).transpose(3, 0, 2, 4, 1)
        l_cyc = l_cyc.reshape(n_amp, ibat * a_chunk, c_local * k_local)
        moved = lax.all_to_all(l_cyc, "amp", split_axis=0, concat_axis=0, tiled=True)
        if t == chunks - 1:
            ladder_chunks[-1] = jnp.dot(
                amplitudes, v_all, precision=HIGHEST, preferred_element_type=jnp.float32
            )
            ladder = jnp.concatenate(ladder_chunks, axis=1)
            moved, ladder = lax.optimization_barrier((moved, ladder))
        moved = moved.reshape(n_amp * ibat * a_chunk, c_local * k_local)
        cycle_chunks.append(
            jnp.dot(moved, w2, precision=HIGHEST, preferred_element_type=jnp.float32)
        )

    parts = jnp.concatenate(
        [c.reshape(n_amp, ibat, sizes[t], columns) for t, c in enumerate(cycle_chunks)], axis=2
    )
    parts = parts.transpose(1, 0, 2, 3).reshape(ibat * slab, columns)
    narrowed = lax.psum_scatter(parts, "amp", scatter_dimension=1, tiled=True)
    sums = lax.psum_scatter(narrowed, "int", scatter_dimension=0, tiled=True)
    col_local = sums.shape[1]

    row_start = lax.axis_index("int") * i_local
    batch_labels = lax.dynamic_slice_in_dim(occ_irrep, row_start, i_local, 0)
    slab_labels = vir_irrep[:slab]
    row_labels = jnp.bitwise_xor(batch_labels[:, None], slab_labels[None, :]).reshape(-1)
    col_ids = lax.axis_index("amp") * col_local + jnp.arange(col_local, dtype=jnp.int32)
    col_occ = col_ids // slab
    col_vir = col_ids % slab
    occ_match = col_occ[:, None] == jnp.arange(nocc, dtype=jnp.int32)[None, :]
    vir_match = col_vir[:, None] == jnp.arange(slab, dtype=jnp.int32)[None, :]
    occ_lookup = jnp.sum(jnp.where(occ_match, occ_irrep[None, :], 0), axis=1)
    vir_lookup = jnp.sum(jnp.where(vir_match, slab_labels[None, :], 0), axis=1)
    col_labels = jnp.bitwise_xor(occ_lookup, vir_lookup)
    keep = row_labels[:, None] == col_labels[None, :]
    cycle = jnp.where(keep, sums, jnp.zeros_like(sums))
    return (ladder, cycle)


def solution(mesh):
    n_amp = mesh.shape["amp"]
    n_int = mesh.shape["int"]
    in_specs = (P("int", None), P("int", "amp"), P("int", "amp", None), P(), P())
    out_specs = (P("int", "amp"), P("int", "amp"))

    def body(*args):
        return per_device(*args, n_amp=n_amp, n_int=n_int)

    return jax.shard_map(
        body, mesh=mesh, in_specs=in_specs, out_specs=out_specs, check_vma=False
    )
```

```python
import jax
import jax.numpy as jnp
from jax import lax
from jax.sharding import PartitionSpec as P

HIGHEST = lax.Precision.HIGHEST
CHUNKS = 3


def per_device(amplitudes, slab_integrals, cycle_integrals, occ_irrep, vir_irrep, n_amp, n_int):
    nocc = occ_irrep.shape[0]
    nvir = vir_irrep.shape[0]
    rows, pw = amplitudes.shape
    pw_local = slab_integrals.shape[0]
    i_local = rows // nocc
    ibat = i_local * n_int
    width = slab_integrals.shape[1]
    a_local = width // nvir
    slab = a_local * n_amp
    k_local, c_local, columns = cycle_integrals.shape
    chunks = min(CHUNKS, a_local)
    sizes = [a_local // chunks + (1 if t < a_local % chunks else 0) for t in range(chunks)]
    starts = [sum(sizes[:t]) for t in range(chunks)]

    t_cyc = lax.all_to_all(
        amplitudes.reshape(i_local, nocc, pw), "int", split_axis=1, concat_axis=0, tiled=True
    ).reshape(ibat * k_local, pw)
    w2 = cycle_integrals.transpose(1, 0, 2).reshape(c_local * k_local, columns)

    slab3 = slab_integrals.reshape(pw_local, a_local, nvir)
    ladder_chunks = []
    cycle_chunks = []
    for t in range(chunks):
        a_chunk = sizes[t]
        v = slab3[:, starts[t]:starts[t] + a_chunk, :].reshape(pw_local, a_chunk * nvir)
        v_all = lax.all_gather(v, "int", axis=0, tiled=True)
        if t:
            v_all, ladder_chunks[-1], cycle_chunks[-1] = lax.optimization_barrier(
                (v_all, ladder_chunks[-1], cycle_chunks[-1])
            )
        ladder_chunks.append(
            jnp.dot(amplitudes, v_all, precision=HIGHEST, preferred_element_type=jnp.float32)
        )
        l_cyc = jnp.dot(t_cyc, v_all, precision=HIGHEST, preferred_element_type=jnp.float32)
        l_cyc = l_cyc.reshape(ibat, k_local, a_chunk, n_amp, c_local).transpose(3, 0, 2, 4, 1)
        l_cyc = l_cyc.reshape(n_amp, ibat * a_chunk, c_local * k_local)
        moved = lax.all_to_all(l_cyc, "amp", split_axis=0, concat_axis=0, tiled=True)
        moved = moved.reshape(n_amp * ibat * a_chunk, c_local * k_local)
        cycle_chunks.append(
            jnp.dot(moved, w2, precision=HIGHEST, preferred_element_type=jnp.float32)
        )
    ladder = jnp.concatenate(ladder_chunks, axis=1)

    parts = jnp.concatenate(
        [c.reshape(n_amp, ibat, sizes[t], columns) for t, c in enumerate(cycle_chunks)], axis=2
    )
    col_local = columns // n_amp
    parts = parts.transpose(1, 0, 2, 3).reshape(n_int, i_local * slab, n_amp, col_local)
    parts = parts.transpose(0, 2, 1, 3).reshape(n_int * n_amp, i_local * slab, col_local)
    gathered = lax.all_to_all(parts, ("int", "amp"), split_axis=0, concat_axis=0, tiled=True)
    sums = jnp.sum(gathered, axis=0)

    row_start = lax.axis_index("int") * i_local
    batch_labels = lax.dynamic_slice_in_dim(occ_irrep, row_start, i_local, 0)
    slab_labels = vir_irrep[:slab]
    row_labels = jnp.bitwise_xor(batch_labels[:, None], slab_labels[None, :]).reshape(-1)
    col_ids = lax.axis_index("amp") * col_local + jnp.arange(col_local, dtype=jnp.int32)
    col_occ = col_ids // slab
    col_vir = col_ids % slab
    occ_match = col_occ[:, None] == jnp.arange(nocc, dtype=jnp.int32)[None, :]
    vir_match = col_vir[:, None] == jnp.arange(slab, dtype=jnp.int32)[None, :]
    occ_lookup = jnp.sum(jnp.where(occ_match, occ_irrep[None, :], 0), axis=1)
    vir_lookup = jnp.sum(jnp.where(vir_match, slab_labels[None, :], 0), axis=1)
    col_labels = jnp.bitwise_xor(occ_lookup, vir_lookup)
    keep = row_labels[:, None] == col_labels[None, :]
    cycle = jnp.where(keep, sums, jnp.zeros_like(sums))
    return (ladder, cycle)


def solution(mesh):
    n_amp = mesh.shape["amp"]
    n_int = mesh.shape["int"]
    in_specs = (P("int", None), P("int", "amp"), P("int", "amp", None), P(), P())
    out_specs = (P("int", "amp"), P("int", "amp"))

    def body(*args):
        return per_device(*args, n_amp=n_amp, n_int=n_int)

    return jax.shard_map(
        body, mesh=mesh, in_specs=in_specs, out_specs=out_specs, check_vma=False
    )
```

```python
import jax
import jax.numpy as jnp
from jax import lax
from jax.sharding import PartitionSpec as P

HIGHEST = lax.Precision.HIGHEST


def per_device(amplitudes, slab_integrals, cycle_integrals, occ_irrep, vir_irrep, n_amp, n_int):
    nocc = occ_irrep.shape[0]
    nvir = vir_irrep.shape[0]
    rows, pw = amplitudes.shape
    pw_local = slab_integrals.shape[0]
    i_local = rows // nocc
    ibat = i_local * n_int
    width = slab_integrals.shape[1]
    a_local = width // nvir
    slab = a_local * n_amp
    k_local, c_local, columns = cycle_integrals.shape
    if a_local >= 4:
        sizes = [a_local // 2, a_local - a_local // 2 - 1, 1]
    elif a_local >= 2:
        sizes = [a_local - 1, 1]
    else:
        sizes = [a_local]
    chunks = len(sizes)
    starts = [sum(sizes[:t]) for t in range(chunks)]

    t_cyc = lax.all_to_all(
        amplitudes.reshape(i_local, nocc, pw), "int", split_axis=1, concat_axis=0, tiled=True
    ).reshape(ibat * k_local, pw)
    w2 = cycle_integrals.transpose(1, 0, 2).reshape(c_local * k_local, columns)

    ladder_chunks = []
    cycle_chunks = []
    for t in range(chunks):
        a_chunk = sizes[t]
        v = lax.slice_in_dim(slab_integrals, starts[t] * nvir, (starts[t] + a_chunk) * nvir, axis=1)
        v_all = lax.all_gather(v, "int", axis=0, tiled=True)
        if t:
            v_all, ladder_chunks[-1], cycle_chunks[-1] = lax.optimization_barrier(
                (v_all, ladder_chunks[-1], cycle_chunks[-1])
            )
        ladder_chunks.append(
            jnp.dot(amplitudes, v_all, precision=HIGHEST, preferred_element_type=jnp.float32)
        )
        l_cyc = jnp.dot(t_cyc, v_all, precision=HIGHEST, preferred_element_type=jnp.float32)
        l_cyc = l_cyc.reshape(ibat, k_local, a_chunk, n_amp, c_local).transpose(3, 0, 2, 4, 1)
        l_cyc = l_cyc.reshape(n_amp, ibat * a_chunk, c_local * k_local)
        moved = lax.all_to_all(l_cyc, "amp", split_axis=0, concat_axis=0, tiled=True)
        moved = moved.reshape(n_amp * ibat * a_chunk, c_local * k_local)
        cycle_chunks.append(
            jnp.dot(moved, w2, precision=HIGHEST, preferred_element_type=jnp.float32)
        )
    ladder = jnp.concatenate(ladder_chunks, axis=1)

    parts = jnp.concatenate(
        [c.reshape(n_amp, ibat, sizes[t], columns) for t, c in enumerate(cycle_chunks)], axis=2
    )
    col_local = columns // n_amp
    parts = parts.transpose(1, 0, 2, 3).reshape(n_int, i_local * slab, n_amp, col_local)
    parts = parts.transpose(0, 2, 1, 3).reshape(n_int * n_amp, i_local * slab, col_local)
    gathered = lax.all_to_all(parts, ("int", "amp"), split_axis=0, concat_axis=0, tiled=True)
    sums = jnp.sum(gathered, axis=0)

    row_start = lax.axis_index("int") * i_local
    batch_labels = lax.dynamic_slice_in_dim(occ_irrep, row_start, i_local, 0)
    slab_labels = vir_irrep[:slab]
    row_labels = jnp.bitwise_xor(batch_labels[:, None], slab_labels[None, :]).reshape(-1)
    col_ids = lax.axis_index("amp") * col_local + jnp.arange(col_local, dtype=jnp.int32)
    col_occ = col_ids // slab
    col_vir = col_ids % slab
    occ_match = col_occ[:, None] == jnp.arange(nocc, dtype=jnp.int32)[None, :]
    vir_match = col_vir[:, None] == jnp.arange(slab, dtype=jnp.int32)[None, :]
    occ_lookup = jnp.sum(jnp.where(occ_match, occ_irrep[None, :], 0), axis=1)
    vir_lookup = jnp.sum(jnp.where(vir_match, slab_labels[None, :], 0), axis=1)
    col_labels = jnp.bitwise_xor(occ_lookup, vir_lookup)
    keep = row_labels[:, None] == col_labels[None, :]
    cycle = jnp.where(keep, sums, jnp.zeros_like(sums))
    return (ladder, cycle)


def solution(mesh):
    n_amp = mesh.shape["amp"]
    n_int = mesh.shape["int"]
    in_specs = (P("int", None), P("int", "amp"), P("int", "amp", None), P(), P())
    out_specs = (P("int", "amp"), P("int", "amp"))

    def body(*args):
        return per_device(*args, n_amp=n_amp, n_int=n_int)

    return jax.shard_map(
        body, mesh=mesh, in_specs=in_specs, out_specs=out_specs, check_vma=False
    )
```

```python
import jax
import jax.numpy as jnp
from jax import lax
from jax.sharding import PartitionSpec as P

HIGHEST = lax.Precision.HIGHEST


def per_device(amplitudes, slab_integrals, cycle_integrals, occ_irrep, vir_irrep, n_amp, n_int):
    nocc = occ_irrep.shape[0]
    nvir = vir_irrep.shape[0]
    rows, pw = amplitudes.shape
    pw_local = slab_integrals.shape[0]
    i_local = rows // nocc
    ibat = i_local * n_int
    width = slab_integrals.shape[1]
    a_local = width // nvir
    slab = a_local * n_amp
    k_local, c_local, columns = cycle_integrals.shape
    if a_local >= 4:
        sizes = [a_local // 2, a_local - a_local // 2 - 1, 1]
    elif a_local >= 2:
        sizes = [a_local - 1, 1]
    else:
        sizes = [a_local]
    chunks = len(sizes)
    starts = [sum(sizes[:t]) for t in range(chunks)]

    t_cyc = lax.all_to_all(
        amplitudes.reshape(i_local, nocc, pw), "int", split_axis=1, concat_axis=0, tiled=True
    ).reshape(ibat * k_local, pw)
    w2 = cycle_integrals.transpose(1, 0, 2).reshape(c_local * k_local, columns)

    def contract(moved, a_chunk):
        part = jnp.dot(moved, w2, precision=HIGHEST, preferred_element_type=jnp.float32)
        part = part.reshape(n_amp, n_int, i_local, a_chunk, n_amp, col_local)
        part = part.transpose(1, 4, 2, 0, 3, 5).reshape(n_int * n_amp, i_local * n_amp * a_chunk, col_local)
        got = lax.all_to_all(part, ("int", "amp"), split_axis=0, concat_axis=0, tiled=True)
        return jnp.sum(got, axis=0).reshape(i_local, n_amp, a_chunk, col_local)

    col_local = columns // n_amp
    ladder_chunks = []
    cycle_chunks = []
    moved = None
    for t in range(chunks):
        a_chunk = sizes[t]
        v = lax.slice_in_dim(slab_integrals, starts[t] * nvir, (starts[t] + a_chunk) * nvir, axis=1)
        v_all = lax.all_gather(v, "int", axis=0, tiled=True)
        if t:
            v_all, ladder_chunks[-1], moved = lax.optimization_barrier((v_all, ladder_chunks[-1], moved))
        l_cyc = jnp.dot(t_cyc, v_all, precision=HIGHEST, preferred_element_type=jnp.float32)
        l_cyc = l_cyc.reshape(ibat, k_local, a_chunk, n_amp, c_local).transpose(3, 0, 2, 4, 1)
        l_cyc = l_cyc.reshape(n_amp, ibat * a_chunk, c_local * k_local)
        moved_next = lax.all_to_all(l_cyc, "amp", split_axis=0, concat_axis=0, tiled=True)
        moved_next = moved_next.reshape(n_amp * ibat * a_chunk, c_local * k_local)
        if t:
            cycle_chunks.append(contract(moved, sizes[t - 1]))
        ladder_chunks.append(
            jnp.dot(amplitudes, v_all, precision=HIGHEST, preferred_element_type=jnp.float32)
        )
        moved = moved_next
    cycle_chunks.append(contract(moved, sizes[-1]))
    ladder = jnp.concatenate(ladder_chunks, axis=1)

    sums = jnp.concatenate(cycle_chunks, axis=2).reshape(i_local * slab, col_local)

    row_start = lax.axis_index("int") * i_local
    batch_labels = lax.dynamic_slice_in_dim(occ_irrep, row_start, i_local, 0)
    slab_labels = vir_irrep[:slab]
    row_labels = jnp.bitwise_xor(batch_labels[:, None], slab_labels[None, :]).reshape(-1)
    col_ids = lax.axis_index("amp") * col_local + jnp.arange(col_local, dtype=jnp.int32)
    col_occ = col_ids // slab
    col_vir = col_ids % slab
    occ_match = col_occ[:, None] == jnp.arange(nocc, dtype=jnp.int32)[None, :]
    vir_match = col_vir[:, None] == jnp.arange(slab, dtype=jnp.int32)[None, :]
    occ_lookup = jnp.sum(jnp.where(occ_match, occ_irrep[None, :], 0), axis=1)
    vir_lookup = jnp.sum(jnp.where(vir_match, slab_labels[None, :], 0), axis=1)
    col_labels = jnp.bitwise_xor(occ_lookup, vir_lookup)
    keep = row_labels[:, None] == col_labels[None, :]
    cycle = jnp.where(keep, sums, jnp.zeros_like(sums))
    return (ladder, cycle)


def solution(mesh):
    n_amp = mesh.shape["amp"]
    n_int = mesh.shape["int"]
    in_specs = (P("int", None), P("int", "amp"), P("int", "amp", None), P(), P())
    out_specs = (P("int", "amp"), P("int", "amp"))

    def body(*args):
        return per_device(*args, n_amp=n_amp, n_int=n_int)

    return jax.shard_map(
        body, mesh=mesh, in_specs=in_specs, out_specs=out_specs, check_vma=False
    )
```

```python
import jax
import jax.numpy as jnp
from jax import lax
from jax.sharding import PartitionSpec as P

PRECISION = lax.Precision.HIGH


def per_device(amplitudes, slab_integrals, cycle_integrals, occ_irrep, vir_irrep, n_amp, n_int):
    nocc = occ_irrep.shape[0]
    nvir = vir_irrep.shape[0]
    rows, pw = amplitudes.shape
    pw_local = slab_integrals.shape[0]
    i_local = rows // nocc
    ibat = i_local * n_int
    width = slab_integrals.shape[1]
    a_local = width // nvir
    slab = a_local * n_amp
    k_local, c_local, columns = cycle_integrals.shape
    if a_local >= 4:
        sizes = [a_local // 2, a_local - a_local // 2 - 1, 1]
    elif a_local >= 2:
        sizes = [a_local - 1, 1]
    else:
        sizes = [a_local]
    chunks = len(sizes)
    starts = [sum(sizes[:t]) for t in range(chunks)]

    t_cyc = lax.all_to_all(
        amplitudes.reshape(i_local, nocc, pw), "int", split_axis=1, concat_axis=0, tiled=True
    ).reshape(ibat * k_local, pw)
    w2 = cycle_integrals.transpose(1, 0, 2).reshape(c_local * k_local, columns)

    ladder_chunks = []
    cycle_chunks = []
    for t in range(chunks):
        a_chunk = sizes[t]
        v = lax.slice_in_dim(slab_integrals, starts[t] * nvir, (starts[t] + a_chunk) * nvir, axis=1)
        v_all = lax.all_gather(v, "int", axis=0, tiled=True)
        if t:
            v_all, ladder_chunks[-1], cycle_chunks[-1] = lax.optimization_barrier(
                (v_all, ladder_chunks[-1], cycle_chunks[-1])
            )
        ladder_chunks.append(
            jnp.dot(amplitudes, v_all, precision=PRECISION, preferred_element_type=jnp.float32)
        )
        l_cyc = jnp.dot(t_cyc, v_all, precision=PRECISION, preferred_element_type=jnp.float32)
        l_cyc = l_cyc.reshape(ibat, k_local, a_chunk, n_amp, c_local).transpose(3, 0, 2, 4, 1)
        l_cyc = l_cyc.reshape(n_amp, ibat * a_chunk, c_local * k_local)
        moved = lax.all_to_all(l_cyc, "amp", split_axis=0, concat_axis=0, tiled=True)
        moved = moved.reshape(n_amp * ibat * a_chunk, c_local * k_local)
        cycle_chunks.append(
            jnp.dot(moved, w2, precision=PRECISION, preferred_element_type=jnp.float32)
        )
    ladder = jnp.concatenate(ladder_chunks, axis=1)

    parts = jnp.concatenate(
        [c.reshape(n_amp, ibat, sizes[t], columns) for t, c in enumerate(cycle_chunks)], axis=2
    )
    col_local = columns // n_amp
    parts = parts.transpose(1, 0, 2, 3).reshape(n_int, i_local * slab, n_amp, col_local)
    parts = parts.transpose(0, 2, 1, 3).reshape(n_int * n_amp, i_local * slab, col_local)
    gathered = lax.all_to_all(parts, ("int", "amp"), split_axis=0, concat_axis=0, tiled=True)
    sums = jnp.sum(gathered, axis=0)

    row_start = lax.axis_index("int") * i_local
    batch_labels = lax.dynamic_slice_in_dim(occ_irrep, row_start, i_local, 0)
    slab_labels = vir_irrep[:slab]
    row_labels = jnp.bitwise_xor(batch_labels[:, None], slab_labels[None, :]).reshape(-1)
    col_ids = lax.axis_index("amp") * col_local + jnp.arange(col_local, dtype=jnp.int32)
    col_occ = col_ids // slab
    col_vir = col_ids % slab
    occ_match = col_occ[:, None] == jnp.arange(nocc, dtype=jnp.int32)[None, :]
    vir_match = col_vir[:, None] == jnp.arange(slab, dtype=jnp.int32)[None, :]
    occ_lookup = jnp.sum(jnp.where(occ_match, occ_irrep[None, :], 0), axis=1)
    vir_lookup = jnp.sum(jnp.where(vir_match, slab_labels[None, :], 0), axis=1)
    col_labels = jnp.bitwise_xor(occ_lookup, vir_lookup)
    keep = row_labels[:, None] == col_labels[None, :]
    cycle = jnp.where(keep, sums, jnp.zeros_like(sums))
    return (ladder, cycle)


def solution(mesh):
    n_amp = mesh.shape["amp"]
    n_int = mesh.shape["int"]
    in_specs = (P("int", None), P("int", "amp"), P("int", "amp", None), P(), P())
    out_specs = (P("int", "amp"), P("int", "amp"))

    def body(*args):
        return per_device(*args, n_amp=n_amp, n_int=n_int)

    return jax.shard_map(
        body, mesh=mesh, in_specs=in_specs, out_specs=out_specs, check_vma=False
    )
```

```python
import jax
import jax.numpy as jnp
from jax import lax
from jax.sharding import PartitionSpec as P

PRECISION = lax.Precision.HIGH


def per_device(amplitudes, slab_integrals, cycle_integrals, occ_irrep, vir_irrep, n_amp, n_int):
    nocc = occ_irrep.shape[0]
    nvir = vir_irrep.shape[0]
    rows, pw = amplitudes.shape
    pw_local = slab_integrals.shape[0]
    i_local = rows // nocc
    ibat = i_local * n_int
    width = slab_integrals.shape[1]
    a_local = width // nvir
    slab = a_local * n_amp
    k_local, c_local, columns = cycle_integrals.shape
    if a_local >= 4:
        sizes = [a_local // 2, a_local - a_local // 2 - 1, 1]
    elif a_local >= 2:
        sizes = [a_local - 1, 1]
    else:
        sizes = [a_local]
    chunks = len(sizes)
    starts = [sum(sizes[:t]) for t in range(chunks)]

    t_cyc = lax.all_to_all(
        amplitudes.reshape(i_local, nocc, pw), "int", split_axis=1, concat_axis=0, tiled=True
    ).reshape(ibat * k_local, pw)
    w2 = cycle_integrals.transpose(1, 0, 2).reshape(c_local * k_local, columns)

    col_local = columns // n_amp

    def reduce_block(part, a_chunk):
        part = part.reshape(n_amp, n_int, i_local, a_chunk, n_amp, col_local)
        part = part.transpose(1, 4, 2, 0, 3, 5).reshape(n_int * n_amp, i_local * n_amp * a_chunk, col_local)
        got = lax.all_to_all(part, ("int", "amp"), split_axis=0, concat_axis=0, tiled=True)
        return jnp.sum(got, axis=0).reshape(i_local, n_amp, a_chunk, col_local)

    ladder_chunks = []
    cycle_chunks = []
    reduced = []
    for t in range(chunks):
        a_chunk = sizes[t]
        v = lax.slice_in_dim(slab_integrals, starts[t] * nvir, (starts[t] + a_chunk) * nvir, axis=1)
        v_all = lax.all_gather(v, "int", axis=0, tiled=True)
        if t == 1:
            v_all, ladder_chunks[-1], reduced[0] = lax.optimization_barrier(
                (v_all, ladder_chunks[-1], reduced[0])
            )
        elif t:
            v_all, ladder_chunks[-1], cycle_chunks[-1] = lax.optimization_barrier(
                (v_all, ladder_chunks[-1], cycle_chunks[-1])
            )
        ladder_chunks.append(None)
        if t < chunks - 1:
            ladder_chunks[-1] = jnp.dot(
                amplitudes, v_all, precision=PRECISION, preferred_element_type=jnp.float32
            )
        l_cyc = jnp.dot(t_cyc, v_all, precision=PRECISION, preferred_element_type=jnp.float32)
        l_cyc = l_cyc.reshape(ibat, k_local, a_chunk, n_amp, c_local).transpose(3, 0, 2, 4, 1)
        l_cyc = l_cyc.reshape(n_amp, ibat * a_chunk, c_local * k_local)
        moved = lax.all_to_all(l_cyc, "amp", split_axis=0, concat_axis=0, tiled=True)
        if t == chunks - 1:
            ladder_chunks[-1] = jnp.dot(
                amplitudes, v_all, precision=PRECISION, preferred_element_type=jnp.float32
            )
            ladder = jnp.concatenate(ladder_chunks, axis=1)
            moved, ladder = lax.optimization_barrier((moved, ladder))
        moved = moved.reshape(n_amp * ibat * a_chunk, c_local * k_local)
        part = jnp.dot(moved, w2, precision=PRECISION, preferred_element_type=jnp.float32)
        if t == 0 and chunks > 1:
            reduced.append(reduce_block(part, a_chunk))
        else:
            cycle_chunks.append(part.reshape(n_amp, ibat, a_chunk, columns))
    rest = jnp.concatenate(cycle_chunks, axis=2)
    reduced.append(reduce_block(rest, rest.shape[2]))

    sums = jnp.concatenate(reduced, axis=2).reshape(i_local * slab, col_local)

    row_start = lax.axis_index("int") * i_local
    batch_labels = lax.dynamic_slice_in_dim(occ_irrep, row_start, i_local, 0)
    slab_labels = vir_irrep[:slab]
    row_labels = jnp.bitwise_xor(batch_labels[:, None], slab_labels[None, :]).reshape(-1)
    col_ids = lax.axis_index("amp") * col_local + jnp.arange(col_local, dtype=jnp.int32)
    col_occ = col_ids // slab
    col_vir = col_ids % slab
    occ_match = col_occ[:, None] == jnp.arange(nocc, dtype=jnp.int32)[None, :]
    vir_match = col_vir[:, None] == jnp.arange(slab, dtype=jnp.int32)[None, :]
    occ_lookup = jnp.sum(jnp.where(occ_match, occ_irrep[None, :], 0), axis=1)
    vir_lookup = jnp.sum(jnp.where(vir_match, slab_labels[None, :], 0), axis=1)
    col_labels = jnp.bitwise_xor(occ_lookup, vir_lookup)
    keep = row_labels[:, None] == col_labels[None, :]
    cycle = jnp.where(keep, sums, jnp.zeros_like(sums))
    return (ladder, cycle)


def solution(mesh):
    n_amp = mesh.shape["amp"]
    n_int = mesh.shape["int"]
    in_specs = (P("int", None), P("int", "amp"), P("int", "amp", None), P(), P())
    out_specs = (P("int", "amp"), P("int", "amp"))

    def body(*args):
        return per_device(*args, n_amp=n_amp, n_int=n_int)

    return jax.shard_map(
        body, mesh=mesh, in_specs=in_specs, out_specs=out_specs, check_vma=False
    )
```

```python
import jax
import jax.numpy as jnp
from jax import lax
from jax.sharding import PartitionSpec as P

PRECISION = lax.Precision.HIGH


def per_device(amplitudes, slab_integrals, cycle_integrals, occ_irrep, vir_irrep, n_amp, n_int):
    nocc = occ_irrep.shape[0]
    nvir = vir_irrep.shape[0]
    rows, pw = amplitudes.shape
    pw_local = slab_integrals.shape[0]
    i_local = rows // nocc
    ibat = i_local * n_int
    width = slab_integrals.shape[1]
    a_local = width // nvir
    slab = a_local * n_amp
    k_local, c_local, columns = cycle_integrals.shape
    if a_local >= 4:
        sizes = [a_local // 2, a_local - a_local // 2 - 1, 1]
    elif a_local >= 2:
        sizes = [a_local - 1, 1]
    else:
        sizes = [a_local]
    chunks = len(sizes)
    starts = [sum(sizes[:t]) for t in range(chunks)]

    t_cyc = lax.all_to_all(
        amplitudes.reshape(i_local, nocc, pw), "int", split_axis=1, concat_axis=0, tiled=True
    ).reshape(ibat * k_local, pw)
    c_pad = -(-c_local // 128) * 128
    if c_pad * 10 > c_local * 13:
        c_pad = c_local
    if c_pad == c_local:
        w2 = cycle_integrals.transpose(1, 0, 2).reshape(c_local * k_local, columns)
    else:
        w2 = jnp.pad(cycle_integrals, ((0, 0), (0, c_pad - c_local), (0, 0)))
        w2 = w2.reshape(k_local * c_pad, columns)

    ladder_chunks = []
    cycle_chunks = []
    for t in range(chunks):
        a_chunk = sizes[t]
        v = lax.slice_in_dim(slab_integrals, starts[t] * nvir, (starts[t] + a_chunk) * nvir, axis=1)
        v_all = lax.all_gather(v, "int", axis=0, tiled=True)
        if t:
            v_all, ladder_chunks[-1], cycle_chunks[-1] = lax.optimization_barrier(
                (v_all, ladder_chunks[-1], cycle_chunks[-1])
            )
        ladder_chunks.append(
            jnp.dot(amplitudes, v_all, precision=PRECISION, preferred_element_type=jnp.float32)
        )
        if c_pad == c_local:
            l_cyc = jnp.dot(t_cyc, v_all, precision=PRECISION, preferred_element_type=jnp.float32)
            l_cyc = l_cyc.reshape(ibat, k_local, a_chunk, n_amp, c_local).transpose(3, 0, 2, 4, 1)
        else:
            v_pad = jnp.pad(
                v_all.reshape(pw, a_chunk, n_amp, c_local),
                ((0, 0), (0, 0), (0, 0), (0, c_pad - c_local)),
            ).reshape(pw, a_chunk * n_amp * c_pad)
            l_cyc = jnp.dot(t_cyc, v_pad, precision=PRECISION, preferred_element_type=jnp.float32)
            l_cyc = l_cyc.reshape(ibat, k_local, a_chunk, n_amp, c_pad).transpose(3, 0, 2, 1, 4)
        l_cyc = l_cyc.reshape(n_amp, ibat * a_chunk, c_pad * k_local)
        moved = lax.all_to_all(l_cyc, "amp", split_axis=0, concat_axis=0, tiled=True)
        moved = moved.reshape(n_amp * ibat * a_chunk, c_pad * k_local)
        cycle_chunks.append(
            jnp.dot(moved, w2, precision=PRECISION, preferred_element_type=jnp.float32)
        )
    ladder = jnp.concatenate(ladder_chunks, axis=1)

    parts = jnp.concatenate(
        [c.reshape(n_amp, ibat, sizes[t], columns) for t, c in enumerate(cycle_chunks)], axis=2
    )
    col_local = columns // n_amp
    parts = parts.transpose(1, 0, 2, 3).reshape(n_int, i_local * slab, n_amp, col_local)
    parts = parts.transpose(0, 2, 1, 3).reshape(n_int * n_amp, i_local * slab, col_local)
    gathered = lax.all_to_all(parts, ("int", "amp"), split_axis=0, concat_axis=0, tiled=True)
    sums = jnp.sum(gathered, axis=0)

    row_start = lax.axis_index("int") * i_local
    batch_labels = lax.dynamic_slice_in_dim(occ_irrep, row_start, i_local, 0)
    slab_labels = vir_irrep[:slab]
    row_labels = jnp.bitwise_xor(batch_labels[:, None], slab_labels[None, :]).reshape(-1)
    col_ids = lax.axis_index("amp") * col_local + jnp.arange(col_local, dtype=jnp.int32)
    col_occ = col_ids // slab
    col_vir = col_ids % slab
    occ_match = col_occ[:, None] == jnp.arange(nocc, dtype=jnp.int32)[None, :]
    vir_match = col_vir[:, None] == jnp.arange(slab, dtype=jnp.int32)[None, :]
    occ_lookup = jnp.sum(jnp.where(occ_match, occ_irrep[None, :], 0), axis=1)
    vir_lookup = jnp.sum(jnp.where(vir_match, slab_labels[None, :], 0), axis=1)
    col_labels = jnp.bitwise_xor(occ_lookup, vir_lookup)
    keep = row_labels[:, None] == col_labels[None, :]
    cycle = jnp.where(keep, sums, jnp.zeros_like(sums))
    return (ladder, cycle)


def solution(mesh):
    n_amp = mesh.shape["amp"]
    n_int = mesh.shape["int"]
    in_specs = (P("int", None), P("int", "amp"), P("int", "amp", None), P(), P())
    out_specs = (P("int", "amp"), P("int", "amp"))

    def body(*args):
        return per_device(*args, n_amp=n_amp, n_int=n_int)

    return jax.shard_map(
        body, mesh=mesh, in_specs=in_specs, out_specs=out_specs, check_vma=False
    )
```

```python
import jax
import jax.numpy as jnp
from jax import lax
from jax.sharding import PartitionSpec as P

PRECISION = lax.Precision.HIGH


def per_device(amplitudes, slab_integrals, cycle_integrals, occ_irrep, vir_irrep, n_amp, n_int):
    nocc = occ_irrep.shape[0]
    nvir = vir_irrep.shape[0]
    rows, pw = amplitudes.shape
    pw_local = slab_integrals.shape[0]
    i_local = rows // nocc
    ibat = i_local * n_int
    width = slab_integrals.shape[1]
    a_local = width // nvir
    slab = a_local * n_amp
    k_local, c_local, columns = cycle_integrals.shape
    if a_local >= 4:
        sizes = [(a_local - 1) // 2, a_local - 2 - (a_local - 1) // 2, 1, 1]
    elif a_local >= 2:
        sizes = [a_local - 1, 1]
    else:
        sizes = [a_local]
    chunks = len(sizes)
    starts = [sum(sizes[:t]) for t in range(chunks)]

    t_cyc = lax.all_to_all(
        amplitudes.reshape(i_local, nocc, pw), "int", split_axis=1, concat_axis=0, tiled=True
    ).reshape(ibat * k_local, pw)
    w2 = cycle_integrals.transpose(1, 0, 2).reshape(c_local * k_local, columns)

    ladder_chunks = []
    cycle_chunks = []
    for t in range(chunks):
        a_chunk = sizes[t]
        v = lax.slice_in_dim(slab_integrals, starts[t] * nvir, (starts[t] + a_chunk) * nvir, axis=1)
        v_all = lax.all_gather(v, "int", axis=0, tiled=True)
        if t:
            v_all, ladder_chunks[-1], cycle_chunks[-1] = lax.optimization_barrier(
                (v_all, ladder_chunks[-1], cycle_chunks[-1])
            )
        ladder_chunks.append(
            jnp.dot(amplitudes, v_all, precision=PRECISION, preferred_element_type=jnp.float32)
        )
        l_cyc = jnp.dot(t_cyc, v_all, precision=PRECISION, preferred_element_type=jnp.float32)
        l_cyc = l_cyc.reshape(ibat, k_local, a_chunk, n_amp, c_local).transpose(3, 0, 2, 4, 1)
        l_cyc = l_cyc.reshape(n_amp, ibat * a_chunk, c_local * k_local)
        moved = lax.all_to_all(l_cyc, "amp", split_axis=0, concat_axis=0, tiled=True)
        moved = moved.reshape(n_amp * ibat * a_chunk, c_local * k_local)
        cycle_chunks.append(
            jnp.dot(moved, w2, precision=PRECISION, preferred_element_type=jnp.float32)
        )
    ladder = jnp.concatenate(ladder_chunks, axis=1)

    parts = jnp.concatenate(
        [c.reshape(n_amp, ibat, sizes[t], columns) for t, c in enumerate(cycle_chunks)], axis=2
    )
    col_local = columns // n_amp
    parts = parts.transpose(1, 0, 2, 3).reshape(n_int, i_local * slab, n_amp, col_local)
    parts = parts.transpose(0, 2, 1, 3).reshape(n_int * n_amp, i_local * slab, col_local)
    gathered = lax.all_to_all(parts, ("int", "amp"), split_axis=0, concat_axis=0, tiled=True)
    sums = jnp.sum(gathered, axis=0)

    row_start = lax.axis_index("int") * i_local
    batch_labels = lax.dynamic_slice_in_dim(occ_irrep, row_start, i_local, 0)
    slab_labels = vir_irrep[:slab]
    row_labels = jnp.bitwise_xor(batch_labels[:, None], slab_labels[None, :]).reshape(-1)
    col_ids = lax.axis_index("amp") * col_local + jnp.arange(col_local, dtype=jnp.int32)
    col_occ = col_ids // slab
    col_vir = col_ids % slab
    occ_match = col_occ[:, None] == jnp.arange(nocc, dtype=jnp.int32)[None, :]
    vir_match = col_vir[:, None] == jnp.arange(slab, dtype=jnp.int32)[None, :]
    occ_lookup = jnp.sum(jnp.where(occ_match, occ_irrep[None, :], 0), axis=1)
    vir_lookup = jnp.sum(jnp.where(vir_match, slab_labels[None, :], 0), axis=1)
    col_labels = jnp.bitwise_xor(occ_lookup, vir_lookup)
    keep = row_labels[:, None] == col_labels[None, :]
    cycle = jnp.where(keep, sums, jnp.zeros_like(sums))
    return (ladder, cycle)


def solution(mesh):
    n_amp = mesh.shape["amp"]
    n_int = mesh.shape["int"]
    in_specs = (P("int", None), P("int", "amp"), P("int", "amp", None), P(), P())
    out_specs = (P("int", "amp"), P("int", "amp"))

    def body(*args):
        return per_device(*args, n_amp=n_amp, n_int=n_int)

    return jax.shard_map(
        body, mesh=mesh, in_specs=in_specs, out_specs=out_specs, check_vma=False
    )
```

```python
import jax
import jax.numpy as jnp
from jax import lax
from jax.sharding import PartitionSpec as P

PRECISION = lax.Precision.HIGH


def per_device(amplitudes, slab_integrals, cycle_integrals, occ_irrep, vir_irrep, n_amp, n_int):
    nocc = occ_irrep.shape[0]
    nvir = vir_irrep.shape[0]
    rows, pw = amplitudes.shape
    pw_local = slab_integrals.shape[0]
    i_local = rows // nocc
    ibat = i_local * n_int
    width = slab_integrals.shape[1]
    a_local = width // nvir
    slab = a_local * n_amp
    k_local, c_local, columns = cycle_integrals.shape
    if a_local >= 4:
        sizes = [(a_local - 1) // 2, a_local - 2 - (a_local - 1) // 2, 1, 1]
    elif a_local >= 2:
        sizes = [a_local - 1, 1]
    else:
        sizes = [a_local]
    chunks = len(sizes)
    starts = [sum(sizes[:t]) for t in range(chunks)]

    t_cyc = lax.all_to_all(
        amplitudes.reshape(i_local, nocc, pw), "int", split_axis=1, concat_axis=0, tiled=True
    ).reshape(ibat * k_local, pw)
    w2 = cycle_integrals.transpose(1, 0, 2).reshape(c_local * k_local, columns)

    col_local = columns // n_amp

    def reduce_block(parts, a_count):
        parts = parts.reshape(n_amp, n_int, i_local, a_count, n_amp, col_local)
        parts = parts.transpose(1, 4, 2, 0, 3, 5).reshape(n_int * n_amp, i_local * n_amp * a_count, col_local)
        got = lax.all_to_all(parts, ("int", "amp"), split_axis=0, concat_axis=0, tiled=True)
        return jnp.sum(got, axis=0).reshape(i_local, n_amp, a_count, col_local)

    ladder_chunks = []
    cycle_chunks = []
    reduced = []
    for t in range(chunks):
        a_chunk = sizes[t]
        v = lax.slice_in_dim(slab_integrals, starts[t] * nvir, (starts[t] + a_chunk) * nvir, axis=1)
        v_all = lax.all_gather(v, "int", axis=0, tiled=True)
        if t and t == chunks - 1:
            early = jnp.concatenate(cycle_chunks, axis=2)
            reduced.append(reduce_block(early, early.shape[2]))
            v_all, ladder_chunks[-1], reduced[0] = lax.optimization_barrier(
                (v_all, ladder_chunks[-1], reduced[0])
            )
        elif t:
            v_all, ladder_chunks[-1], cycle_chunks[-1] = lax.optimization_barrier(
                (v_all, ladder_chunks[-1], cycle_chunks[-1])
            )
        ladder_chunks.append(
            jnp.dot(amplitudes, v_all, precision=PRECISION, preferred_element_type=jnp.float32)
        )
        l_cyc = jnp.dot(t_cyc, v_all, precision=PRECISION, preferred_element_type=jnp.float32)
        l_cyc = l_cyc.reshape(ibat, k_local, a_chunk, n_amp, c_local).transpose(3, 0, 2, 4, 1)
        l_cyc = l_cyc.reshape(n_amp, ibat * a_chunk, c_local * k_local)
        moved = lax.all_to_all(l_cyc, "amp", split_axis=0, concat_axis=0, tiled=True)
        moved = moved.reshape(n_amp * ibat * a_chunk, c_local * k_local)
        part = jnp.dot(moved, w2, precision=PRECISION, preferred_element_type=jnp.float32)
        cycle_chunks.append(part.reshape(n_amp, ibat, a_chunk, columns))
    ladder = jnp.concatenate(ladder_chunks, axis=1)
    reduced.append(reduce_block(cycle_chunks[-1], sizes[-1]))

    sums = jnp.concatenate(reduced, axis=2).reshape(i_local * slab, col_local)

    row_start = lax.axis_index("int") * i_local
    batch_labels = lax.dynamic_slice_in_dim(occ_irrep, row_start, i_local, 0)
    slab_labels = vir_irrep[:slab]
    row_labels = jnp.bitwise_xor(batch_labels[:, None], slab_labels[None, :]).reshape(-1)
    col_ids = lax.axis_index("amp") * col_local + jnp.arange(col_local, dtype=jnp.int32)
    col_occ = col_ids // slab
    col_vir = col_ids % slab
    occ_match = col_occ[:, None] == jnp.arange(nocc, dtype=jnp.int32)[None, :]
    vir_match = col_vir[:, None] == jnp.arange(slab, dtype=jnp.int32)[None, :]
    occ_lookup = jnp.sum(jnp.where(occ_match, occ_irrep[None, :], 0), axis=1)
    vir_lookup = jnp.sum(jnp.where(vir_match, slab_labels[None, :], 0), axis=1)
    col_labels = jnp.bitwise_xor(occ_lookup, vir_lookup)
    keep = row_labels[:, None] == col_labels[None, :]
    cycle = jnp.where(keep, sums, jnp.zeros_like(sums))
    return (ladder, cycle)


def solution(mesh):
    n_amp = mesh.shape["amp"]
    n_int = mesh.shape["int"]
    in_specs = (P("int", None), P("int", "amp"), P("int", "amp", None), P(), P())
    out_specs = (P("int", "amp"), P("int", "amp"))

    def body(*args):
        return per_device(*args, n_amp=n_amp, n_int=n_int)

    return jax.shard_map(
        body, mesh=mesh, in_specs=in_specs, out_specs=out_specs, check_vma=False
    )
```

```python
import jax
import jax.numpy as jnp
from jax import lax
from jax.sharding import PartitionSpec as P

PRECISION = lax.Precision.HIGH


def per_device(amplitudes, slab_integrals, cycle_integrals, occ_irrep, vir_irrep, n_amp, n_int):
    nocc = occ_irrep.shape[0]
    nvir = vir_irrep.shape[0]
    rows, pw = amplitudes.shape
    pw_local = slab_integrals.shape[0]
    i_local = rows // nocc
    ibat = i_local * n_int
    width = slab_integrals.shape[1]
    a_local = width // nvir
    slab = a_local * n_amp
    k_local, c_local, columns = cycle_integrals.shape
    if a_local >= 4:
        sizes = [a_local - 3, 2, 1]
    elif a_local >= 2:
        sizes = [a_local - 1, 1]
    else:
        sizes = [a_local]
    chunks = len(sizes)
    starts = [sum(sizes[:t]) for t in range(chunks)]

    t_cyc = lax.all_to_all(
        amplitudes.reshape(i_local, nocc, pw), "int", split_axis=1, concat_axis=0, tiled=True
    ).reshape(ibat * k_local, pw)
    w2 = cycle_integrals.transpose(1, 0, 2).reshape(c_local * k_local, columns)

    ladder_chunks = []
    cycle_chunks = []
    for t in range(chunks):
        a_chunk = sizes[t]
        v = lax.slice_in_dim(slab_integrals, starts[t] * nvir, (starts[t] + a_chunk) * nvir, axis=1)
        v_all = lax.all_gather(v, "int", axis=0, tiled=True)
        if t:
            v_all, ladder_chunks[-1], cycle_chunks[-1] = lax.optimization_barrier(
                (v_all, ladder_chunks[-1], cycle_chunks[-1])
            )
        ladder_chunks.append(
            jnp.dot(amplitudes, v_all, precision=PRECISION, preferred_element_type=jnp.float32)
        )
        l_cyc = jnp.dot(t_cyc, v_all, precision=PRECISION, preferred_element_type=jnp.float32)
        l_cyc = l_cyc.reshape(ibat, k_local, a_chunk, n_amp, c_local).transpose(3, 0, 2, 4, 1)
        l_cyc = l_cyc.reshape(n_amp, ibat * a_chunk, c_local * k_local)
        moved = lax.all_to_all(l_cyc, "amp", split_axis=0, concat_axis=0, tiled=True)
        moved = moved.reshape(n_amp * ibat * a_chunk, c_local * k_local)
        cycle_chunks.append(
            jnp.dot(moved, w2, precision=PRECISION, preferred_element_type=jnp.float32)
        )
    ladder = jnp.concatenate(ladder_chunks, axis=1)

    parts = jnp.concatenate(
        [c.reshape(n_amp, ibat, sizes[t], columns) for t, c in enumerate(cycle_chunks)], axis=2
    )
    col_local = columns // n_amp
    parts = parts.transpose(1, 0, 2, 3).reshape(n_int, i_local * slab, n_amp, col_local)
    parts = parts.transpose(0, 2, 1, 3).reshape(n_int * n_amp, i_local * slab, col_local)
    gathered = lax.all_to_all(parts, ("int", "amp"), split_axis=0, concat_axis=0, tiled=True)
    sums = jnp.sum(gathered, axis=0)

    row_start = lax.axis_index("int") * i_local
    batch_labels = lax.dynamic_slice_in_dim(occ_irrep, row_start, i_local, 0)
    slab_labels = vir_irrep[:slab]
    row_labels = jnp.bitwise_xor(batch_labels[:, None], slab_labels[None, :]).reshape(-1)
    col_ids = lax.axis_index("amp") * col_local + jnp.arange(col_local, dtype=jnp.int32)
    col_occ = col_ids // slab
    col_vir = col_ids % slab
    occ_match = col_occ[:, None] == jnp.arange(nocc, dtype=jnp.int32)[None, :]
    vir_match = col_vir[:, None] == jnp.arange(slab, dtype=jnp.int32)[None, :]
    occ_lookup = jnp.sum(jnp.where(occ_match, occ_irrep[None, :], 0), axis=1)
    vir_lookup = jnp.sum(jnp.where(vir_match, slab_labels[None, :], 0), axis=1)
    col_labels = jnp.bitwise_xor(occ_lookup, vir_lookup)
    keep = row_labels[:, None] == col_labels[None, :]
    cycle = jnp.where(keep, sums, jnp.zeros_like(sums))
    return (ladder, cycle)


def solution(mesh):
    n_amp = mesh.shape["amp"]
    n_int = mesh.shape["int"]
    in_specs = (P("int", None), P("int", "amp"), P("int", "amp", None), P(), P())
    out_specs = (P("int", "amp"), P("int", "amp"))

    def body(*args):
        return per_device(*args, n_amp=n_amp, n_int=n_int)

    return jax.shard_map(
        body, mesh=mesh, in_specs=in_specs, out_specs=out_specs, check_vma=False
    )
```

```python
import jax
import jax.numpy as jnp
from jax import lax
from jax.sharding import PartitionSpec as P

PRECISION = lax.Precision.HIGH


def per_device(amplitudes, slab_integrals, cycle_integrals, occ_irrep, vir_irrep, n_amp, n_int):
    nocc = occ_irrep.shape[0]
    nvir = vir_irrep.shape[0]
    rows, pw = amplitudes.shape
    pw_local = slab_integrals.shape[0]
    i_local = rows // nocc
    ibat = i_local * n_int
    width = slab_integrals.shape[1]
    a_local = width // nvir
    slab = a_local * n_amp
    k_local, c_local, columns = cycle_integrals.shape
    if a_local >= 4:
        sizes = [(a_local - 1) // 2, a_local - 2 - (a_local - 1) // 2, 1, 1]
    elif a_local >= 2:
        sizes = [a_local - 1, 1]
    else:
        sizes = [a_local]
    chunks = len(sizes)
    starts = [sum(sizes[:t]) for t in range(chunks)]

    t_cyc = lax.all_to_all(
        amplitudes.reshape(i_local, nocc, pw), "int", split_axis=1, concat_axis=0, tiled=True
    ).reshape(ibat * k_local, pw)
    w2 = cycle_integrals.transpose(1, 0, 2).reshape(c_local * k_local, columns)

    ladder_chunks = []
    cycle_chunks = []
    for t in range(chunks):
        a_chunk = sizes[t]
        v = lax.slice_in_dim(slab_integrals, starts[t] * nvir, (starts[t] + a_chunk) * nvir, axis=1)
        v_all = lax.all_gather(v, "int", axis=0, tiled=True)
        if t:
            v_all, ladder_chunks[-1], cycle_chunks[-1] = lax.optimization_barrier(
                (v_all, ladder_chunks[-1], cycle_chunks[-1])
            )
        ladder_chunks.append(
            jnp.dot(amplitudes, v_all, precision=PRECISION, preferred_element_type=jnp.float32)
        )
        l_cyc = jnp.dot(t_cyc, v_all, precision=PRECISION, preferred_element_type=jnp.float32)
        l_cyc = l_cyc.reshape(ibat, k_local, a_chunk, n_amp, c_local).transpose(3, 0, 2, 4, 1)
        l_cyc = l_cyc.reshape(n_amp, ibat * a_chunk, c_local * k_local)
        moved = lax.all_to_all(l_cyc, "amp", split_axis=0, concat_axis=0, tiled=True)
        moved = moved.reshape(n_amp * ibat * a_chunk, c_local * k_local)
        cycle_chunks.append(
            jnp.dot(moved, w2, precision=PRECISION, preferred_element_type=jnp.float32)
        )
    ladder = jnp.concatenate(ladder_chunks, axis=1)

    parts = jnp.concatenate(
        [c.reshape(n_amp, ibat, sizes[t], columns) for t, c in enumerate(cycle_chunks)], axis=2
    )
    col_local = columns // n_amp
    parts = parts.reshape(n_amp, ibat, a_local, n_amp, col_local).transpose(3, 0, 1, 2, 4)
    parts = jnp.sum(lax.all_to_all(parts, "amp", split_axis=0, concat_axis=0, tiled=True), axis=0)
    parts = parts.reshape(n_amp, n_int, i_local, a_local, col_local).transpose(1, 2, 0, 3, 4)
    parts = jnp.sum(lax.all_to_all(parts, "int", split_axis=0, concat_axis=0, tiled=True), axis=0)
    sums = parts.reshape(i_local * slab, col_local)

    row_start = lax.axis_index("int") * i_local
    batch_labels = lax.dynamic_slice_in_dim(occ_irrep, row_start, i_local, 0)
    slab_labels = vir_irrep[:slab]
    row_labels = jnp.bitwise_xor(batch_labels[:, None], slab_labels[None, :]).reshape(-1)
    col_ids = lax.axis_index("amp") * col_local + jnp.arange(col_local, dtype=jnp.int32)
    col_occ = col_ids // slab
    col_vir = col_ids % slab
    occ_match = col_occ[:, None] == jnp.arange(nocc, dtype=jnp.int32)[None, :]
    vir_match = col_vir[:, None] == jnp.arange(slab, dtype=jnp.int32)[None, :]
    occ_lookup = jnp.sum(jnp.where(occ_match, occ_irrep[None, :], 0), axis=1)
    vir_lookup = jnp.sum(jnp.where(vir_match, slab_labels[None, :], 0), axis=1)
    col_labels = jnp.bitwise_xor(occ_lookup, vir_lookup)
    keep = row_labels[:, None] == col_labels[None, :]
    cycle = jnp.where(keep, sums, jnp.zeros_like(sums))
    return (ladder, cycle)


def solution(mesh):
    n_amp = mesh.shape["amp"]
    n_int = mesh.shape["int"]
    in_specs = (P("int", None), P("int", "amp"), P("int", "amp", None), P(), P())
    out_specs = (P("int", "amp"), P("int", "amp"))

    def body(*args):
        return per_device(*args, n_amp=n_amp, n_int=n_int)

    return jax.shard_map(
        body, mesh=mesh, in_specs=in_specs, out_specs=out_specs, check_vma=False
    )
```

```python
import jax
import jax.numpy as jnp
from jax import lax
from jax.sharding import PartitionSpec as P

PRECISION = lax.Precision.HIGH


def per_device(amplitudes, slab_integrals, cycle_integrals, occ_irrep, vir_irrep, n_amp, n_int):
    nocc = occ_irrep.shape[0]
    nvir = vir_irrep.shape[0]
    rows, pw = amplitudes.shape
    pw_local = slab_integrals.shape[0]
    i_local = rows // nocc
    ibat = i_local * n_int
    width = slab_integrals.shape[1]
    a_local = width // nvir
    slab = a_local * n_amp
    k_local, c_local, columns = cycle_integrals.shape
    if a_local >= 4:
        sizes = [(a_local - 1) // 2, a_local - 2 - (a_local - 1) // 2, 1, 1]
    elif a_local >= 2:
        sizes = [a_local - 1, 1]
    else:
        sizes = [a_local]
    chunks = len(sizes)
    starts = [sum(sizes[:t]) for t in range(chunks)]

    t_cyc = lax.all_to_all(
        amplitudes.reshape(i_local, nocc, pw), "int", split_axis=1, concat_axis=0, tiled=True
    ).reshape(ibat * k_local, pw)
    w2 = cycle_integrals.transpose(1, 0, 2).reshape(c_local * k_local, columns)

    ladder_chunks = []
    cycle_chunks = []
    pending = None
    for t in range(chunks):
        a_chunk = sizes[t]
        v = lax.slice_in_dim(slab_integrals, starts[t] * nvir, (starts[t] + a_chunk) * nvir, axis=1)
        v_all = lax.all_gather(v, "int", axis=0, tiled=True)
        if t and pending is not None:
            v_all, ladder_chunks[-1], pending = lax.optimization_barrier((v_all, ladder_chunks[-1], pending))
        elif t:
            v_all, ladder_chunks[-1], cycle_chunks[-1] = lax.optimization_barrier(
                (v_all, ladder_chunks[-1], cycle_chunks[-1])
            )
        ladder_chunks.append(
            jnp.dot(amplitudes, v_all, precision=PRECISION, preferred_element_type=jnp.float32)
        )
        l_cyc = jnp.dot(t_cyc, v_all, precision=PRECISION, preferred_element_type=jnp.float32)
        l_cyc = l_cyc.reshape(ibat, k_local, a_chunk, n_amp, c_local).transpose(3, 0, 2, 4, 1)
        l_cyc = l_cyc.reshape(n_amp, ibat * a_chunk, c_local * k_local)
        moved = lax.all_to_all(l_cyc, "amp", split_axis=0, concat_axis=0, tiled=True)
        moved = moved.reshape(n_amp * ibat * a_chunk, c_local * k_local)
        if pending is not None:
            cycle_chunks.append(
                jnp.dot(pending, w2, precision=PRECISION, preferred_element_type=jnp.float32)
            )
            pending = None
        if t == chunks - 2:
            pending = moved
        else:
            cycle_chunks.append(
                jnp.dot(moved, w2, precision=PRECISION, preferred_element_type=jnp.float32)
            )
    ladder = jnp.concatenate(ladder_chunks, axis=1)

    parts = jnp.concatenate(
        [c.reshape(n_amp, ibat, sizes[t], columns) for t, c in enumerate(cycle_chunks)], axis=2
    )
    col_local = columns // n_amp
    parts = parts.transpose(1, 0, 2, 3).reshape(n_int, i_local * slab, n_amp, col_local)
    parts = parts.transpose(0, 2, 1, 3).reshape(n_int * n_amp, i_local * slab, col_local)
    gathered = lax.all_to_all(parts, ("int", "amp"), split_axis=0, concat_axis=0, tiled=True)
    sums = jnp.sum(gathered, axis=0)

    row_start = lax.axis_index("int") * i_local
    batch_labels = lax.dynamic_slice_in_dim(occ_irrep, row_start, i_local, 0)
    slab_labels = vir_irrep[:slab]
    row_labels = jnp.bitwise_xor(batch_labels[:, None], slab_labels[None, :]).reshape(-1)
    col_ids = lax.axis_index("amp") * col_local + jnp.arange(col_local, dtype=jnp.int32)
    col_occ = col_ids // slab
    col_vir = col_ids % slab
    occ_match = col_occ[:, None] == jnp.arange(nocc, dtype=jnp.int32)[None, :]
    vir_match = col_vir[:, None] == jnp.arange(slab, dtype=jnp.int32)[None, :]
    occ_lookup = jnp.sum(jnp.where(occ_match, occ_irrep[None, :], 0), axis=1)
    vir_lookup = jnp.sum(jnp.where(vir_match, slab_labels[None, :], 0), axis=1)
    col_labels = jnp.bitwise_xor(occ_lookup, vir_lookup)
    keep = row_labels[:, None] == col_labels[None, :]
    cycle = jnp.where(keep, sums, jnp.zeros_like(sums))
    return (ladder, cycle)


def solution(mesh):
    n_amp = mesh.shape["amp"]
    n_int = mesh.shape["int"]
    in_specs = (P("int", None), P("int", "amp"), P("int", "amp", None), P(), P())
    out_specs = (P("int", "amp"), P("int", "amp"))

    def body(*args):
        return per_device(*args, n_amp=n_amp, n_int=n_int)

    return jax.shard_map(
        body, mesh=mesh, in_specs=in_specs, out_specs=out_specs, check_vma=False
    )
```

```python
import jax
import jax.numpy as jnp
from jax import lax
from jax.sharding import PartitionSpec as P

PRECISION = lax.Precision.HIGH


def per_device(amplitudes, slab_integrals, cycle_integrals, occ_irrep, vir_irrep, n_amp, n_int):
    nocc = occ_irrep.shape[0]
    nvir = vir_irrep.shape[0]
    rows, pw = amplitudes.shape
    pw_local = slab_integrals.shape[0]
    i_local = rows // nocc
    ibat = i_local * n_int
    width = slab_integrals.shape[1]
    a_local = width // nvir
    slab = a_local * n_amp
    k_local, c_local, columns = cycle_integrals.shape
    if a_local >= 4:
        sizes = [(a_local - 1) // 2, a_local - 2 - (a_local - 1) // 2, 1, 1]
    elif a_local >= 2:
        sizes = [a_local - 1, 1]
    else:
        sizes = [a_local]
    chunks = len(sizes)
    starts = [sum(sizes[:t]) for t in range(chunks)]

    if pw % n_amp == 0:
        piece = pw // n_amp
        mine = lax.dynamic_slice_in_dim(amplitudes, lax.axis_index("amp") * piece, piece, axis=1)
        mine = lax.all_to_all(
            mine.reshape(i_local, nocc, piece), "int", split_axis=1, concat_axis=0, tiled=True
        )
        copies = jnp.broadcast_to(mine[None], (n_amp, ibat, k_local, piece))
        t_cyc = lax.all_to_all(copies, "amp", split_axis=0, concat_axis=3, tiled=True)
        t_cyc = t_cyc.reshape(ibat * k_local, pw)
    else:
        t_cyc = lax.all_to_all(
            amplitudes.reshape(i_local, nocc, pw), "int", split_axis=1, concat_axis=0, tiled=True
        ).reshape(ibat * k_local, pw)
    w2 = cycle_integrals.transpose(1, 0, 2).reshape(c_local * k_local, columns)

    ladder_chunks = []
    cycle_chunks = []
    for t in range(chunks):
        a_chunk = sizes[t]
        v = lax.slice_in_dim(slab_integrals, starts[t] * nvir, (starts[t] + a_chunk) * nvir, axis=1)
        v_all = lax.all_gather(v, "int", axis=0, tiled=True)
        if t:
            v_all, ladder_chunks[-1], cycle_chunks[-1] = lax.optimization_barrier(
                (v_all, ladder_chunks[-1], cycle_chunks[-1])
            )
        ladder_chunks.append(
            jnp.dot(amplitudes, v_all, precision=PRECISION, preferred_element_type=jnp.float32)
        )
        l_cyc = jnp.dot(t_cyc, v_all, precision=PRECISION, preferred_element_type=jnp.float32)
        l_cyc = l_cyc.reshape(ibat, k_local, a_chunk, n_amp, c_local).transpose(3, 0, 2, 4, 1)
        l_cyc = l_cyc.reshape(n_amp, ibat * a_chunk, c_local * k_local)
        moved = lax.all_to_all(l_cyc, "amp", split_axis=0, concat_axis=0, tiled=True)
        moved = moved.reshape(n_amp * ibat * a_chunk, c_local * k_local)
        cycle_chunks.append(
            jnp.dot(moved, w2, precision=PRECISION, preferred_element_type=jnp.float32)
        )
    ladder = jnp.concatenate(ladder_chunks, axis=1)

    parts = jnp.concatenate(
        [c.reshape(n_amp, ibat, sizes[t], columns) for t, c in enumerate(cycle_chunks)], axis=2
    )
    col_local = columns // n_amp
    parts = parts.transpose(1, 0, 2, 3).reshape(n_int, i_local * slab, n_amp, col_local)
    parts = parts.transpose(0, 2, 1, 3).reshape(n_int * n_amp, i_local * slab, col_local)
    gathered = lax.all_to_all(parts, ("int", "amp"), split_axis=0, concat_axis=0, tiled=True)
    sums = jnp.sum(gathered, axis=0)

    row_start = lax.axis_index("int") * i_local
    batch_labels = lax.dynamic_slice_in_dim(occ_irrep, row_start, i_local, 0)
    slab_labels = vir_irrep[:slab]
    row_labels = jnp.bitwise_xor(batch_labels[:, None], slab_labels[None, :]).reshape(-1)
    col_ids = lax.axis_index("amp") * col_local + jnp.arange(col_local, dtype=jnp.int32)
    col_occ = col_ids // slab
    col_vir = col_ids % slab
    occ_match = col_occ[:, None] == jnp.arange(nocc, dtype=jnp.int32)[None, :]
    vir_match = col_vir[:, None] == jnp.arange(slab, dtype=jnp.int32)[None, :]
    occ_lookup = jnp.sum(jnp.where(occ_match, occ_irrep[None, :], 0), axis=1)
    vir_lookup = jnp.sum(jnp.where(vir_match, slab_labels[None, :], 0), axis=1)
    col_labels = jnp.bitwise_xor(occ_lookup, vir_lookup)
    keep = row_labels[:, None] == col_labels[None, :]
    cycle = jnp.where(keep, sums, jnp.zeros_like(sums))
    return (ladder, cycle)


def solution(mesh):
    n_amp = mesh.shape["amp"]
    n_int = mesh.shape["int"]
    in_specs = (P("int", None), P("int", "amp"), P("int", "amp", None), P(), P())
    out_specs = (P("int", "amp"), P("int", "amp"))

    def body(*args):
        return per_device(*args, n_amp=n_amp, n_int=n_int)

    return jax.shard_map(
        body, mesh=mesh, in_specs=in_specs, out_specs=out_specs, check_vma=False
    )
```

```python
import jax
import jax.numpy as jnp
from jax import lax
from jax.sharding import PartitionSpec as P

PRECISION = lax.Precision.HIGH


def per_device(amplitudes, slab_integrals, cycle_integrals, occ_irrep, vir_irrep, n_amp, n_int):
    nocc = occ_irrep.shape[0]
    nvir = vir_irrep.shape[0]
    rows, pw = amplitudes.shape
    pw_local = slab_integrals.shape[0]
    i_local = rows // nocc
    ibat = i_local * n_int
    width = slab_integrals.shape[1]
    a_local = width // nvir
    slab = a_local * n_amp
    k_local, c_local, columns = cycle_integrals.shape
    if a_local >= 4:
        sizes = [(a_local - 1) // 2, a_local - 2 - (a_local - 1) // 2, 1, 1]
    elif a_local >= 2:
        sizes = [a_local - 1, 1]
    else:
        sizes = [a_local]
    chunks = len(sizes)
    starts = [sum(sizes[:t]) for t in range(chunks)]

    t_cyc = lax.all_to_all(
        amplitudes.reshape(i_local, nocc, pw), "int", split_axis=1, concat_axis=0, tiled=True
    ).reshape(ibat * k_local, pw)
    w2 = cycle_integrals.transpose(1, 0, 2).reshape(c_local * k_local, columns)

    ladder_chunks = []
    cycle_chunks = []
    for t in range(chunks):
        a_chunk = sizes[t]
        v = lax.slice_in_dim(slab_integrals, starts[t] * nvir, (starts[t] + a_chunk) * nvir, axis=1)
        v_all = lax.all_gather(v, "int", axis=0, tiled=True)
        if t:
            v_all, ladder_chunks[-1], cycle_chunks[-1] = lax.optimization_barrier(
                (v_all, ladder_chunks[-1], cycle_chunks[-1])
            )
        ladder_chunks.append(
            jnp.dot(amplitudes, v_all, precision=PRECISION, preferred_element_type=jnp.float32)
        )
        l_cyc = jnp.dot(t_cyc, v_all, precision=PRECISION, preferred_element_type=jnp.float32)
        l_cyc = l_cyc.reshape(ibat, k_local, a_chunk, n_amp, c_local).transpose(3, 0, 2, 4, 1)
        l_cyc = l_cyc.reshape(n_amp, ibat * a_chunk, c_local * k_local)
        moved = lax.all_to_all(l_cyc, "amp", split_axis=0, concat_axis=0, tiled=True)
        moved = moved.reshape(n_amp * ibat * a_chunk, c_local * k_local)
        cycle_chunks.append(
            jnp.dot(moved, w2, precision=PRECISION, preferred_element_type=jnp.float32)
        )
    ladder = jnp.concatenate(ladder_chunks, axis=1)

    parts = jnp.concatenate(
        [c.reshape(n_amp, ibat, sizes[t], columns) for t, c in enumerate(cycle_chunks)], axis=2
    )
    col_local = columns // n_amp
    parts = parts.transpose(1, 0, 2, 3).reshape(n_int, i_local * slab, n_amp, col_local)
    parts = parts.transpose(0, 2, 1, 3).reshape(n_int * n_amp, i_local * slab, col_local)
    gathered = lax.all_to_all(parts, ("int", "amp"), split_axis=0, concat_axis=0, tiled=True)
    sums = jnp.sum(gathered, axis=0)

    labels = jnp.bitwise_xor(occ_irrep[:ibat, None], vir_irrep[None, :slab]).reshape(-1)
    rows_local = i_local * slab
    row_labels = lax.dynamic_slice_in_dim(labels, lax.axis_index("int") * rows_local, rows_local, 0)
    col_labels = lax.dynamic_slice_in_dim(labels, lax.axis_index("amp") * col_local, col_local, 0)
    keep = row_labels[:, None] == col_labels[None, :]
    cycle = jnp.where(keep, sums, jnp.zeros_like(sums))
    return (ladder, cycle)


def solution(mesh):
    n_amp = mesh.shape["amp"]
    n_int = mesh.shape["int"]
    in_specs = (P("int", None), P("int", "amp"), P("int", "amp", None), P(), P())
    out_specs = (P("int", "amp"), P("int", "amp"))

    def body(*args):
        return per_device(*args, n_amp=n_amp, n_int=n_int)

    return jax.shard_map(
        body, mesh=mesh, in_specs=in_specs, out_specs=out_specs, check_vma=False
    )
```

```python
import jax
import jax.numpy as jnp
from jax import lax
from jax.sharding import PartitionSpec as P

PRECISION = lax.Precision.HIGH


def per_device(amplitudes, slab_integrals, cycle_integrals, occ_irrep, vir_irrep, n_amp, n_int):
    nocc = occ_irrep.shape[0]
    nvir = vir_irrep.shape[0]
    rows, pw = amplitudes.shape
    pw_local = slab_integrals.shape[0]
    i_local = rows // nocc
    ibat = i_local * n_int
    width = slab_integrals.shape[1]
    a_local = width // nvir
    slab = a_local * n_amp
    k_local, c_local, columns = cycle_integrals.shape
    if a_local >= 4:
        sizes = [(a_local - 1) // 2, a_local - 2 - (a_local - 1) // 2, 1, 1]
    elif a_local >= 2:
        sizes = [a_local - 1, 1]
    else:
        sizes = [a_local]
    chunks = len(sizes)
    starts = [sum(sizes[:t]) for t in range(chunks)]

    t_cyc = lax.all_to_all(
        amplitudes.reshape(i_local, nocc, pw), "int", split_axis=1, concat_axis=0, tiled=True
    ).reshape(ibat * k_local, pw)
    w2 = cycle_integrals.transpose(1, 0, 2).reshape(c_local * k_local, columns)

    ladder_chunks = []
    cycle_chunks = []
    pending = None
    for t in range(chunks):
        a_chunk = sizes[t]
        v = lax.slice_in_dim(slab_integrals, starts[t] * nvir, (starts[t] + a_chunk) * nvir, axis=1)
        v_all = lax.all_gather(v, "int", axis=0, tiled=True)
        if t and pending is not None:
            v_all, ladder_chunks[-1], pending = lax.optimization_barrier((v_all, ladder_chunks[-1], pending))
        elif t:
            v_all, ladder_chunks[-1], cycle_chunks[-1] = lax.optimization_barrier(
                (v_all, ladder_chunks[-1], cycle_chunks[-1])
            )
        ladder_chunks.append(
            jnp.dot(amplitudes, v_all, precision=PRECISION, preferred_element_type=jnp.float32)
        )
        l_cyc = jnp.dot(t_cyc, v_all, precision=PRECISION, preferred_element_type=jnp.float32)
        l_cyc = l_cyc.reshape(ibat, k_local, a_chunk, n_amp, c_local).transpose(3, 0, 2, 4, 1)
        l_cyc = l_cyc.reshape(n_amp, ibat * a_chunk, c_local * k_local)
        moved = lax.all_to_all(l_cyc, "amp", split_axis=0, concat_axis=0, tiled=True)
        moved = moved.reshape(n_amp * ibat * a_chunk, c_local * k_local)
        if pending is not None:
            cycle_chunks.append(
                jnp.dot(pending, w2, precision=PRECISION, preferred_element_type=jnp.float32)
            )
            pending = None
        if t == chunks - 2:
            pending = moved
        else:
            cycle_chunks.append(
                jnp.dot(moved, w2, precision=PRECISION, preferred_element_type=jnp.float32)
            )
    ladder = jnp.concatenate(ladder_chunks, axis=1)

    parts = jnp.concatenate(
        [c.reshape(n_amp, ibat, sizes[t], columns) for t, c in enumerate(cycle_chunks)], axis=2
    )
    col_local = columns // n_amp
    parts = parts.transpose(1, 0, 2, 3).reshape(n_int, i_local * slab, n_amp, col_local)
    parts = parts.transpose(0, 2, 1, 3).reshape(n_int * n_amp, i_local * slab, col_local)
    gathered = lax.all_to_all(parts, ("int", "amp"), split_axis=0, concat_axis=0, tiled=True)
    sums = jnp.sum(gathered, axis=0)

    labels = jnp.bitwise_xor(occ_irrep[:ibat, None], vir_irrep[None, :slab]).reshape(-1)
    rows_local = i_local * slab
    row_labels = lax.dynamic_slice_in_dim(labels, lax.axis_index("int") * rows_local, rows_local, 0)
    col_labels = lax.dynamic_slice_in_dim(labels, lax.axis_index("amp") * col_local, col_local, 0)
    keep = row_labels[:, None] == col_labels[None, :]
    cycle = jnp.where(keep, sums, jnp.zeros_like(sums))
    return (ladder, cycle)


def solution(mesh):
    n_amp = mesh.shape["amp"]
    n_int = mesh.shape["int"]
    in_specs = (P("int", None), P("int", "amp"), P("int", "amp", None), P(), P())
    out_specs = (P("int", "amp"), P("int", "amp"))

    def body(*args):
        return per_device(*args, n_amp=n_amp, n_int=n_int)

    return jax.shard_map(
        body, mesh=mesh, in_specs=in_specs, out_specs=out_specs, check_vma=False
    )
```
